256 devices in a mesh: dp: 32 (over z_lo, x, core), mp: 8 (over z_hi, y).
Axes of the slice: x: 4, y: 4, z: 8 (z_hi: 2, z_lo: 4; z = z_hi * 4 + z_lo), core: 2. Of those that a mesh axis runs over, the one named last changes fastest.
Arguments:
- tokens_in: bfloat16 [8192, 8192], P('dp', 'mp'), may hold values from -6 to 6
- grad_out: bfloat16 [8192, 8192], P('dp', 'mp'), may hold values from -6 to 6
- gate_in: bfloat16 [64, 128, 128], P('mp'), may hold values from -0.5 to 0.5
- gate_out: bfloat16 [64, 128, 448], P('mp'), may hold values from -0.5 to 0.5
- up_in: bfloat16 [64, 128, 128], P('mp'), may hold values from -0.5 to 0.5
- up_out: bfloat16 [64, 128, 448], P('mp'), may hold values from -0.5 to 0.5
- down_in: bfloat16 [64, 448, 128], P('mp'), may hold values from -0.25 to 0.25
- down_out: bfloat16 [64, 128, 128], P('mp'), may hold values from -0.5 to 0.5
Outputs:
- grad_x: bfloat16 [8192, 8192], P('dp', 'mp')
- grad_gate_in: float32 [64, 128, 128], P('mp', 'dp')
- grad_gate_out: float32 [64, 128, 448], P('mp', 'dp')
- grad_up_in: float32 [64, 128, 128], P('mp', 'dp')
- grad_up_out: float32 [64, 128, 448], P('mp', 'dp')
- grad_down_in: float32 [64, 448, 128], P('mp', 'dp')
- grad_down_out: float32 [64, 128, 128], P('mp', 'dp')
The draws below stay inside these ranges and needn't reach their ends.
All inputs are finite; a program needn't handle non-finite values.
Results may differ from the reference program's by a relative error of at most 0.0072.
Values may be sent and summed in bfloat16 or wider, within the bound.
No kernel may reach another device: no remote copies, remote signals or barrier semaphores. Data moves between devices by JAX's collectives and lax.ppermute only.
A program may use at most 64 MiB of HBM per device.

```python
import math
import jax
import jax.numpy as jnp
from jax import lax

D = 8192
BLK = 128
TOKENS = 8192
NBLK = 64
PAIR = 2
FBLK = 448


def block_scale(key, dims, shards, smallest, top_value):
    gain, own = 1.0, jax.random.fold_in(key, 6)
    for position, blocks in shards:
        steps = jnp.exp(jax.random.uniform(jax.random.fold_in(own, position), (blocks,), jnp.float32, smallest / len(shards), top_value / len(shards)))
        gain = gain * jnp.repeat(steps, dims[position] // blocks).reshape([-1 if axis == position else 1 for axis in range(len(dims))])
    return gain


def noise(own_key, shape, spread, most, cuts=(), kind=jnp.bfloat16):
    array = spread * jax.random.normal(own_key, shape, jnp.float32)
    if cuts:
        array = array * block_scale(own_key, shape, cuts, -0.22, 0.18)
    return jnp.clip(array, -most, most).astype(kind)


def setup_inputs(seed: int = 0) -> dict:
    splits = jax.random.split(jax.random.key(seed), 9)
    tokens_in = noise(splits[0], (TOKENS, D), 1.0, 6.0, ((0, 32), (1, 8)))
    grad_out = noise(splits[1], (TOKENS, D), 1.0, 6.0, ((0, 32), (1, 8)))
    gate_in = noise(splits[2], (NBLK, BLK, BLK), BLK ** -0.5, 0.5, ((0, 8),))
    gate_out = noise(splits[3], (NBLK, BLK, FBLK), BLK ** -0.5, 0.5, ((0, 8),))
    up_in = noise(splits[4], (NBLK, BLK, BLK), BLK ** -0.5, 0.5, ((0, 8),))
    up_out = noise(splits[5], (NBLK, BLK, FBLK), BLK ** -0.5, 0.5, ((0, 8),))
    down_in = noise(splits[6], (NBLK, FBLK, BLK), FBLK ** -0.5, 0.25, ((0, 8),))
    down_out = noise(splits[7], (NBLK, BLK, BLK), BLK ** -0.5, 0.5, ((0, 8),))
    return dict(tokens_in=tokens_in, grad_out=grad_out, gate_in=gate_in, gate_out=gate_out, up_in=up_in, up_out=up_out, down_in=down_in, down_out=down_out)


def permute(values):
    rows = values.shape[0]
    return values.reshape(rows, NBLK, NBLK, PAIR).transpose(0, 2, 1, 3).reshape(rows, NBLK, BLK)

def block_product(values, weight):
    return jnp.einsum('tki,kio->tko', values.astype(jnp.float32), weight.astype(jnp.float32))

def outer_sum(left, right):
    return jnp.einsum('tki,tko->kio', left.astype(jnp.float32), right.astype(jnp.float32))

def reference(tokens_in, grad_out, gate_in, gate_out, up_in, up_out, down_in, down_out):
    block_rows = math.gcd(TOKENS, 1024)
    count = TOKENS // block_rows
    scale = 1.0 / math.sqrt(TOKENS)
    x_all = tokens_in.reshape(count, block_rows, NBLK, BLK)
    dy_all = grad_out.reshape(count, block_rows, NBLK, BLK)

    def one_block(carry, pieces):
        x_blocks, dy_blocks = pieces
        gate_mid = permute(block_product(x_blocks, gate_in).astype(jnp.bfloat16))
        up_mid = permute(block_product(x_blocks, up_in).astype(jnp.bfloat16))
        gate_pre = block_product(gate_mid, gate_out)
        up_pre = block_product(up_mid, up_out)
        sigmoid_gate = jax.nn.sigmoid(gate_pre)
        activated = gate_pre * sigmoid_gate
        hidden = (activated * up_pre).astype(jnp.bfloat16)
        down_mid = permute(block_product(hidden, down_in).astype(jnp.bfloat16))
        term_down_out = outer_sum(down_mid, dy_blocks)
        back_mid = permute(block_product(dy_blocks, down_out.transpose(0, 2, 1)).astype(jnp.bfloat16))
        term_down_in = outer_sum(hidden, back_mid)
        hidden_grad = block_product(back_mid, down_in.transpose(0, 2, 1))
        gate_grad = (hidden_grad * up_pre * sigmoid_gate * (1.0 + gate_pre * (1.0 - sigmoid_gate))).astype(jnp.bfloat16)
        up_grad = (hidden_grad * activated).astype(jnp.bfloat16)
        term_gate_out = outer_sum(gate_mid, gate_grad)
        term_up_out = outer_sum(up_mid, up_grad)
        gate_back = permute(block_product(gate_grad, gate_out.transpose(0, 2, 1)).astype(jnp.bfloat16))
        up_back = permute(block_product(up_grad, up_out.transpose(0, 2, 1)).astype(jnp.bfloat16))
        term_gate_in = outer_sum(x_blocks, gate_back)
        term_up_in = outer_sum(x_blocks, up_back)
        input_grad = block_product(gate_back, gate_in.transpose(0, 2, 1)) + block_product(up_back, up_in.transpose(0, 2, 1))
        input_grad = input_grad.astype(jnp.bfloat16).reshape(block_rows, D)
        terms = (term_gate_in, term_gate_out, term_up_in, term_up_out, term_down_in, term_down_out)
        carry = tuple((total + term for total, term in zip(carry, terms)))
        return (carry, input_grad)
    start = (jnp.zeros((NBLK, BLK, BLK), jnp.float32), jnp.zeros((NBLK, BLK, FBLK), jnp.float32), jnp.zeros((NBLK, BLK, BLK), jnp.float32), jnp.zeros((NBLK, BLK, FBLK), jnp.float32), jnp.zeros((NBLK, FBLK, BLK), jnp.float32), jnp.zeros((NBLK, BLK, BLK), jnp.float32))
    totals, grad_pieces = lax.scan(one_block, start, (x_all, dy_all))
    grad_x = grad_pieces.reshape(TOKENS, D)
    return (grad_x, totals[0] * scale, totals[1] * scale, totals[2] * scale, totals[3] * scale, totals[4] * scale, totals[5] * scale)
```

```python
import math

import jax
import jax.numpy as jnp
from jax import lax
from jax.sharding import PartitionSpec as P

BLK = 128
NBLK = 64
PAIR = 2
FBLK = 448


def shards(tokens_in, grad_out, gate_in, gate_out, up_in, up_out, down_in, down_out):
    local_blocks = gate_in.shape[0]
    rows = tokens_in.shape[0]
    scale = 1.0 / math.sqrt(rows * lax.axis_size("dp"))
    x_blocks = tokens_in.reshape(rows, local_blocks, BLK)
    dy_blocks = grad_out.reshape(rows, local_blocks, BLK)

    def mix_in(weight):
        shaped = weight.reshape(local_blocks, BLK, NBLK, PAIR)
        spread = jnp.einsum("tki,kijp->jkpt", x_blocks, shaped, preferred_element_type=jnp.float32)
        return spread.astype(jnp.bfloat16).reshape(NBLK, local_blocks * PAIR, rows)

    def widen(mixed, weight):
        return jnp.einsum("jct,jco->jot", mixed, weight, preferred_element_type=jnp.float32)

    gate_mid = mix_in(gate_in)
    up_mid = mix_in(up_in)
    back_shaped = down_out.reshape(local_blocks, NBLK, PAIR, BLK)
    back_mid = jnp.einsum(
        "tkr,kjpr->jkpt", dy_blocks, back_shaped, preferred_element_type=jnp.float32
    )
    back_mid = back_mid.astype(jnp.bfloat16).reshape(NBLK, local_blocks * PAIR, rows)
    first_recv = lax.all_to_all(
        jnp.stack([gate_mid, up_mid, back_mid]), "mp", split_axis=1, concat_axis=2, tiled=True
    )
    gate_recv, up_recv, back_recv = first_recv[0], first_recv[1], first_recv[2]
    gate_pre = widen(gate_recv, gate_out)
    up_pre = widen(up_recv, up_out)
    sigmoid_gate = jax.nn.sigmoid(gate_pre)
    activated = gate_pre * sigmoid_gate
    hidden = (activated * up_pre).astype(jnp.bfloat16)
    down_shaped = down_in.reshape(local_blocks, FBLK, NBLK, PAIR)
    down_mid = jnp.einsum("jot,jokp->kjpt", hidden, down_shaped, preferred_element_type=jnp.float32)
    down_mid = down_mid.astype(jnp.bfloat16).reshape(NBLK, local_blocks * PAIR, rows)
    down_recv = lax.all_to_all(down_mid, "mp", split_axis=0, concat_axis=1, tiled=True)
    term_down_out = jnp.einsum(
        "kct,tkr->kcr", down_recv, dy_blocks, preferred_element_type=jnp.float32
    )
    term_down_in = jnp.einsum("jot,jqt->joq", hidden, back_recv, preferred_element_type=jnp.float32)
    hidden_grad = jnp.einsum("joq,jqt->jot", down_in, back_recv, preferred_element_type=jnp.float32)
    gate_grad = (
        hidden_grad * up_pre * sigmoid_gate * (1.0 + gate_pre * (1.0 - sigmoid_gate))
    ).astype(jnp.bfloat16)
    up_grad = (hidden_grad * activated).astype(jnp.bfloat16)
    term_gate_out = jnp.einsum(
        "jct,jot->jco", gate_recv, gate_grad, preferred_element_type=jnp.float32
    )
    term_up_out = jnp.einsum("jct,jot->jco", up_recv, up_grad, preferred_element_type=jnp.float32)

    def narrow(grad, weight):
        shaped = weight.reshape(local_blocks, NBLK, PAIR, FBLK)
        spread = jnp.einsum("jot,jkpo->kjpt", grad, shaped, preferred_element_type=jnp.float32)
        return spread.astype(jnp.bfloat16).reshape(NBLK, local_blocks * PAIR, rows)

    back_recv2 = lax.all_to_all(
        jnp.stack([narrow(gate_grad, gate_out), narrow(up_grad, up_out)]),
        "mp", split_axis=1, concat_axis=2, tiled=True,
    )
    gate_back, up_back = back_recv2[0], back_recv2[1]
    input_grad = jnp.einsum("kio,kot->tki", gate_in, gate_back, preferred_element_type=jnp.float32)
    input_grad = input_grad + jnp.einsum(
        "kio,kot->tki", up_in, up_back, preferred_element_type=jnp.float32
    )
    term_gate_in = jnp.einsum(
        "tki,kot->kio", x_blocks, gate_back, preferred_element_type=jnp.float32
    )
    term_up_in = jnp.einsum("tki,kot->kio", x_blocks, up_back, preferred_element_type=jnp.float32)
    grad_x = input_grad.astype(jnp.bfloat16).reshape(rows, local_blocks * BLK)
    terms = (term_gate_in, term_gate_out, term_up_in, term_up_out, term_down_in, term_down_out)
    groups = lax.axis_size("dp")
    flat = [term.reshape(term.shape[0], groups, -1) for term in terms]
    widths = [piece.shape[2] for piece in flat]
    summed = lax.psum_scatter(
        jnp.concatenate(flat, axis=2), "dp", scatter_dimension=1, tiled=True
    )
    outs = []
    start = 0
    for term, width in zip(terms, widths):
        piece = summed[:, 0, start:start + width]
        start += width
        outs.append(piece.reshape(term.shape[0], term.shape[1] // groups, term.shape[2]) * scale)
    return (grad_x, *outs)


def solution(mesh):
    in_specs = (
        P("dp", "mp"),
        P("dp", "mp"),
        P("mp", None, None),
        P("mp", None, None),
        P("mp", None, None),
        P("mp", None, None),
        P("mp", None, None),
        P("mp", None, None),
    )
    out_specs = (
        P("dp", "mp"),
        P("mp", "dp", None),
        P("mp", "dp", None),
        P("mp", "dp", None),
        P("mp", "dp", None),
        P("mp", "dp", None),
        P("mp", "dp", None),
    )
    return jax.shard_map(shards, mesh=mesh, in_specs=in_specs, out_specs=out_specs, check_vma=False)
```

```python
import math

import jax
import jax.numpy as jnp
from jax import lax
from jax.sharding import Mesh, PartitionSpec as P

BLK = 128
NBLK = 64
PAIR = 2
FBLK = 448
DP = ("dz", "dx", "dc")


def shards(tokens_in, grad_out, gate_in, gate_out, up_in, up_out, down_in, down_out):
    local_blocks = gate_in.shape[0]
    rows = tokens_in.shape[0]
    groups = lax.axis_size(DP)
    scale = 1.0 / math.sqrt(rows * groups)
    x_blocks = tokens_in.reshape(rows, local_blocks, BLK)
    dy_blocks = grad_out.reshape(rows, local_blocks, BLK)

    def mix_in(weight):
        shaped = weight.reshape(local_blocks, BLK, NBLK, PAIR)
        spread = jnp.einsum("tki,kijp->jkpt", x_blocks, shaped, preferred_element_type=jnp.float32)
        return spread.astype(jnp.bfloat16).reshape(NBLK, local_blocks * PAIR, rows)

    def widen(mixed, weight):
        return jnp.einsum("jct,jco->jot", mixed, weight, preferred_element_type=jnp.float32)

    gate_mid = mix_in(gate_in)
    up_mid = mix_in(up_in)
    back_shaped = down_out.reshape(local_blocks, NBLK, PAIR, BLK)
    back_mid = jnp.einsum(
        "tkr,kjpr->jkpt", dy_blocks, back_shaped, preferred_element_type=jnp.float32
    )
    back_mid = back_mid.astype(jnp.bfloat16).reshape(NBLK, local_blocks * PAIR, rows)
    first_recv = lax.all_to_all(
        jnp.stack([gate_mid, up_mid, back_mid]), "mp", split_axis=1, concat_axis=2, tiled=True
    )
    gate_recv, up_recv, back_recv = first_recv[0], first_recv[1], first_recv[2]
    gate_pre = widen(gate_recv, gate_out)
    up_pre = widen(up_recv, up_out)
    sigmoid_gate = jax.nn.sigmoid(gate_pre)
    activated = gate_pre * sigmoid_gate
    hidden = (activated * up_pre).astype(jnp.bfloat16)
    down_shaped = down_in.reshape(local_blocks, FBLK, NBLK, PAIR)
    down_mid = jnp.einsum("jot,jokp->kjpt", hidden, down_shaped, preferred_element_type=jnp.float32)
    down_mid = down_mid.astype(jnp.bfloat16).reshape(NBLK, local_blocks * PAIR, rows)
    down_recv = lax.all_to_all(down_mid, "mp", split_axis=0, concat_axis=1, tiled=True)
    term_down_out = jnp.einsum(
        "kct,tkr->kcr", down_recv, dy_blocks, preferred_element_type=jnp.float32
    )
    term_down_in = jnp.einsum("jot,jqt->joq", hidden, back_recv, preferred_element_type=jnp.float32)
    hidden_grad = jnp.einsum("joq,jqt->jot", down_in, back_recv, preferred_element_type=jnp.float32)
    gate_grad = (
        hidden_grad * up_pre * sigmoid_gate * (1.0 + gate_pre * (1.0 - sigmoid_gate))
    ).astype(jnp.bfloat16)
    up_grad = (hidden_grad * activated).astype(jnp.bfloat16)
    term_gate_out = jnp.einsum(
        "jct,jot->jco", gate_recv, gate_grad, preferred_element_type=jnp.float32
    )
    term_up_out = jnp.einsum("jct,jot->jco", up_recv, up_grad, preferred_element_type=jnp.float32)

    def narrow(grad, weight):
        shaped = weight.reshape(local_blocks, NBLK, PAIR, FBLK)
        spread = jnp.einsum("jot,jkpo->kjpt", grad, shaped, preferred_element_type=jnp.float32)
        return spread.astype(jnp.bfloat16).reshape(NBLK, local_blocks * PAIR, rows)

    back_recv2 = lax.all_to_all(
        jnp.stack([narrow(gate_grad, gate_out), narrow(up_grad, up_out)]),
        "mp", split_axis=1, concat_axis=2, tiled=True,
    )
    gate_back, up_back = back_recv2[0], back_recv2[1]
    input_grad = jnp.einsum("kio,kot->tki", gate_in, gate_back, preferred_element_type=jnp.float32)
    input_grad = input_grad + jnp.einsum(
        "kio,kot->tki", up_in, up_back, preferred_element_type=jnp.float32
    )
    term_gate_in = jnp.einsum(
        "tki,kot->kio", x_blocks, gate_back, preferred_element_type=jnp.float32
    )
    term_up_in = jnp.einsum("tki,kot->kio", x_blocks, up_back, preferred_element_type=jnp.float32)
    grad_x = input_grad.astype(jnp.bfloat16).reshape(rows, local_blocks * BLK)
    terms = (term_gate_in, term_gate_out, term_up_in, term_up_out, term_down_in, term_down_out)
    flat = [term.reshape(term.shape[0], groups, -1) for term in terms]
    widths = [piece.shape[2] for piece in flat]
    stacked = jnp.concatenate(flat, axis=2)
    sizes = [lax.axis_size(name) for name in DP]
    summed = stacked.reshape(stacked.shape[0], *sizes, stacked.shape[2])
    for position in reversed(range(len(DP))):
        summed = lax.psum_scatter(summed, DP[position], scatter_dimension=1 + position, tiled=True)
    summed = summed.reshape(stacked.shape[0], 1, stacked.shape[2])
    outs = []
    start = 0
    for term, width in zip(terms, widths):
        piece = summed[:, 0, start:start + width]
        start += width
        outs.append(piece.reshape(term.shape[0], term.shape[1] // groups, term.shape[2]) * scale)
    return (grad_x, *outs)


def solution(mesh):
    dp = mesh.shape["dp"]
    mp = mesh.shape["mp"]
    sub = (dp // 8, 4, 2) if dp % 8 == 0 else (dp,)
    fine = Mesh(mesh.devices.reshape(*sub, mp), DP[-len(sub):] + ("mp",))
    names = DP[-len(sub):]
    in_specs = (
        P(names, "mp"),
        P(names, "mp"),
        P("mp", None, None),
        P("mp", None, None),
        P("mp", None, None),
        P("mp", None, None),
        P("mp", None, None),
        P("mp", None, None),
    )
    out_specs = (
        P(names, "mp"),
        P("mp", names, None),
        P("mp", names, None),
        P("mp", names, None),
        P("mp", names, None),
        P("mp", names, None),
        P("mp", names, None),
    )
    return jax.shard_map(shards, mesh=fine, in_specs=in_specs, out_specs=out_specs, check_vma=False)
```

```python
import math

import jax
import jax.numpy as jnp
from jax import lax
from jax.sharding import Mesh, PartitionSpec as P

BLK = 128
NBLK = 64
PAIR = 2
FBLK = 448
DP = ("dz", "dx", "dc")


def shards(tokens_in, grad_out, gate_in, gate_out, up_in, up_out, down_in, down_out):
    local_blocks = gate_in.shape[0]
    rows = tokens_in.shape[0]
    groups = lax.axis_size(DP)
    scale = 1.0 / math.sqrt(rows * groups)
    x_blocks = tokens_in.reshape(rows, local_blocks, BLK)
    dy_blocks = grad_out.reshape(rows, local_blocks, BLK)

    def mix_in(weight):
        shaped = weight.reshape(local_blocks, BLK, NBLK, PAIR)
        spread = jnp.einsum("tki,kijp->jkpt", x_blocks, shaped, preferred_element_type=jnp.float32)
        return spread.astype(jnp.bfloat16).reshape(NBLK, local_blocks * PAIR, rows)

    def widen(mixed, weight):
        return jnp.einsum("jct,jco->jot", mixed, weight, preferred_element_type=jnp.float32)

    gate_mid = mix_in(gate_in)
    up_mid = mix_in(up_in)
    back_shaped = down_out.reshape(local_blocks, NBLK, PAIR, BLK)
    back_mid = jnp.einsum(
        "tkr,kjpr->jkpt", dy_blocks, back_shaped, preferred_element_type=jnp.float32
    )
    back_mid = back_mid.astype(jnp.bfloat16).reshape(NBLK, local_blocks * PAIR, rows)
    first_recv = lax.all_to_all(
        jnp.stack([gate_mid, up_mid, back_mid]), "mp", split_axis=1, concat_axis=2, tiled=True
    )
    gate_recv, up_recv, back_recv = first_recv[0], first_recv[1], first_recv[2]
    gate_pre = widen(gate_recv, gate_out)
    up_pre = widen(up_recv, up_out)
    sigmoid_gate = jax.nn.sigmoid(gate_pre)
    activated = gate_pre * sigmoid_gate
    hidden = (activated * up_pre).astype(jnp.bfloat16)
    down_shaped = down_in.reshape(local_blocks, FBLK, NBLK, PAIR)
    down_mid = jnp.einsum("jot,jokp->kjpt", hidden, down_shaped, preferred_element_type=jnp.float32)
    down_mid = down_mid.astype(jnp.bfloat16).reshape(NBLK, local_blocks * PAIR, rows)
    down_recv = lax.all_to_all(down_mid, "mp", split_axis=0, concat_axis=1, tiled=True)
    term_down_out = jnp.einsum(
        "kct,tkr->kcr", down_recv, dy_blocks, preferred_element_type=jnp.float32
    )
    term_down_in = jnp.einsum("jot,jqt->joq", hidden, back_recv, preferred_element_type=jnp.float32)
    hidden_grad = jnp.einsum("joq,jqt->jot", down_in, back_recv, preferred_element_type=jnp.float32)
    gate_grad = (
        hidden_grad * up_pre * sigmoid_gate * (1.0 + gate_pre * (1.0 - sigmoid_gate))
    ).astype(jnp.bfloat16)
    up_grad = (hidden_grad * activated).astype(jnp.bfloat16)
    term_gate_out = jnp.einsum(
        "jct,jot->jco", gate_recv, gate_grad, preferred_element_type=jnp.float32
    )
    term_up_out = jnp.einsum("jct,jot->jco", up_recv, up_grad, preferred_element_type=jnp.float32)

    def narrow(grad, weight):
        shaped = weight.reshape(local_blocks, NBLK, PAIR, FBLK)
        spread = jnp.einsum("jot,jkpo->kjpt", grad, shaped, preferred_element_type=jnp.float32)
        return spread.astype(jnp.bfloat16).reshape(NBLK, local_blocks * PAIR, rows)

    back_recv2 = lax.all_to_all(
        jnp.stack([narrow(gate_grad, gate_out), narrow(up_grad, up_out)]),
        "mp", split_axis=1, concat_axis=2, tiled=True,
    )
    gate_back, up_back = back_recv2[0], back_recv2[1]
    input_grad = jnp.einsum("kio,kot->tki", gate_in, gate_back, preferred_element_type=jnp.float32)
    input_grad = input_grad + jnp.einsum(
        "kio,kot->tki", up_in, up_back, preferred_element_type=jnp.float32
    )
    term_gate_in = jnp.einsum(
        "tki,kot->kio", x_blocks, gate_back, preferred_element_type=jnp.float32
    )
    term_up_in = jnp.einsum("tki,kot->kio", x_blocks, up_back, preferred_element_type=jnp.float32)
    grad_x = input_grad.astype(jnp.bfloat16).reshape(rows, local_blocks * BLK)
    terms = (term_gate_in, term_gate_out, term_up_in, term_up_out, term_down_in, term_down_out)
    flat = [term.reshape(term.shape[0], groups, -1) for term in terms]
    widths = [piece.shape[2] for piece in flat]
    stacked = jnp.concatenate(flat, axis=2)
    sizes = [lax.axis_size(name) for name in DP]
    summed = stacked.reshape(stacked.shape[0], *sizes, stacked.shape[2])
    for position in reversed(range(len(DP))):
        summed = lax.all_to_all(
            summed, DP[position], split_axis=1 + position, concat_axis=1 + position, tiled=True
        ).sum(axis=1 + position, keepdims=True)
    summed = summed.reshape(stacked.shape[0], 1, stacked.shape[2])
    outs = []
    start = 0
    for term, width in zip(terms, widths):
        piece = summed[:, 0, start:start + width]
        start += width
        outs.append(piece.reshape(term.shape[0], term.shape[1] // groups, term.shape[2]) * scale)
    return (grad_x, *outs)


def solution(mesh):
    dp = mesh.shape["dp"]
    mp = mesh.shape["mp"]
    sub = (dp // 8, 4, 2) if dp % 8 == 0 else (dp,)
    fine = Mesh(mesh.devices.reshape(*sub, mp), DP[-len(sub):] + ("mp",))
    names = DP[-len(sub):]
    in_specs = (
        P(names, "mp"),
        P(names, "mp"),
        P("mp", None, None),
        P("mp", None, None),
        P("mp", None, None),
        P("mp", None, None),
        P("mp", None, None),
        P("mp", None, None),
    )
    out_specs = (
        P(names, "mp"),
        P("mp", names, None),
        P("mp", names, None),
        P("mp", names, None),
        P("mp", names, None),
        P("mp", names, None),
        P("mp", names, None),
    )
    return jax.shard_map(shards, mesh=fine, in_specs=in_specs, out_specs=out_specs, check_vma=False)
```

```python
import math

import jax
import jax.numpy as jnp
from jax import lax
from jax.sharding import Mesh, PartitionSpec as P

BLK = 128
NBLK = 64
PAIR = 2
FBLK = 448
DP = ("dz", "dx", "dc")


def shards(tokens_in, grad_out, gate_in, gate_out, up_in, up_out, down_in, down_out):
    local_blocks = gate_in.shape[0]
    rows = tokens_in.shape[0]
    groups = lax.axis_size(DP)
    scale = 1.0 / math.sqrt(rows * groups)
    x_blocks = tokens_in.reshape(rows, local_blocks, BLK)
    dy_blocks = grad_out.reshape(rows, local_blocks, BLK)

    def mix_in(weight):
        shaped = weight.reshape(local_blocks, BLK, NBLK, PAIR)
        spread = jnp.einsum("tki,kijp->jkpt", x_blocks, shaped, preferred_element_type=jnp.float32)
        return spread.astype(jnp.bfloat16).reshape(NBLK, local_blocks * PAIR, rows)

    def widen(mixed, weight):
        return jnp.einsum("jct,jco->jot", mixed, weight, preferred_element_type=jnp.float32)

    gate_mid = mix_in(gate_in)
    up_mid = mix_in(up_in)
    back_shaped = down_out.reshape(local_blocks, NBLK, PAIR, BLK)
    back_mid = jnp.einsum(
        "tkr,kjpr->jkpt", dy_blocks, back_shaped, preferred_element_type=jnp.float32
    )
    back_mid = back_mid.astype(jnp.bfloat16).reshape(NBLK, local_blocks * PAIR, rows)
    first_recv = lax.all_to_all(
        jnp.stack([gate_mid, up_mid, back_mid]), "mp", split_axis=1, concat_axis=2, tiled=True
    )
    gate_recv, up_recv, back_recv = first_recv[0], first_recv[1], first_recv[2]
    gate_pre = widen(gate_recv, gate_out)
    up_pre = widen(up_recv, up_out)
    sigmoid_gate = jax.nn.sigmoid(gate_pre)
    activated = gate_pre * sigmoid_gate
    hidden = (activated * up_pre).astype(jnp.bfloat16)
    down_shaped = down_in.reshape(local_blocks, FBLK, NBLK, PAIR)
    down_mid = jnp.einsum("jot,jokp->kjpt", hidden, down_shaped, preferred_element_type=jnp.float32)
    down_mid = down_mid.astype(jnp.bfloat16).reshape(NBLK, local_blocks * PAIR, rows)
    down_recv = lax.all_to_all(down_mid, "mp", split_axis=0, concat_axis=1, tiled=True)
    term_down_out = jnp.einsum(
        "kct,tkr->kcr", down_recv, dy_blocks, preferred_element_type=jnp.float32
    )
    term_down_in = jnp.einsum("jot,jqt->joq", hidden, back_recv, preferred_element_type=jnp.float32)
    hidden_grad = jnp.einsum("joq,jqt->jot", down_in, back_recv, preferred_element_type=jnp.float32)
    gate_grad = (
        hidden_grad * up_pre * sigmoid_gate * (1.0 + gate_pre * (1.0 - sigmoid_gate))
    ).astype(jnp.bfloat16)
    up_grad = (hidden_grad * activated).astype(jnp.bfloat16)
    term_gate_out = jnp.einsum(
        "jct,jot->jco", gate_recv, gate_grad, preferred_element_type=jnp.float32
    )
    term_up_out = jnp.einsum("jct,jot->jco", up_recv, up_grad, preferred_element_type=jnp.float32)

    def narrow(grad, weight):
        shaped = weight.reshape(local_blocks, NBLK, PAIR, FBLK)
        spread = jnp.einsum("jot,jkpo->kjpt", grad, shaped, preferred_element_type=jnp.float32)
        return spread.astype(jnp.bfloat16).reshape(NBLK, local_blocks * PAIR, rows)

    back_recv2 = lax.all_to_all(
        jnp.stack([narrow(gate_grad, gate_out), narrow(up_grad, up_out)]),
        "mp", split_axis=1, concat_axis=2, tiled=True,
    )
    gate_back, up_back = back_recv2[0], back_recv2[1]
    input_grad = jnp.einsum("kio,kot->tki", gate_in, gate_back, preferred_element_type=jnp.float32)
    input_grad = input_grad + jnp.einsum(
        "kio,kot->tki", up_in, up_back, preferred_element_type=jnp.float32
    )
    term_gate_in = jnp.einsum(
        "tki,kot->kio", x_blocks, gate_back, preferred_element_type=jnp.float32
    )
    term_up_in = jnp.einsum("tki,kot->kio", x_blocks, up_back, preferred_element_type=jnp.float32)
    grad_x = input_grad.astype(jnp.bfloat16).reshape(rows, local_blocks * BLK)
    terms = (term_gate_in, term_gate_out, term_up_in, term_up_out, term_down_in, term_down_out)
    flat = [term.reshape(term.shape[0], groups, -1) for term in terms]
    widths = [piece.shape[2] for piece in flat]
    stacked = jnp.concatenate(flat, axis=2)
    sizes = [lax.axis_size(name) for name in DP]
    summed = stacked.reshape(stacked.shape[0], *sizes, stacked.shape[2])
    for position in reversed(range(len(DP))):
        wire = summed if position == len(DP) - 1 else summed.astype(jnp.bfloat16)
        summed = lax.all_to_all(
            wire, DP[position], split_axis=1 + position, concat_axis=1 + position, tiled=True
        ).astype(jnp.float32).sum(axis=1 + position, keepdims=True)
    summed = summed.reshape(stacked.shape[0], 1, stacked.shape[2])
    outs = []
    start = 0
    for term, width in zip(terms, widths):
        piece = summed[:, 0, start:start + width]
        start += width
        outs.append(piece.reshape(term.shape[0], term.shape[1] // groups, term.shape[2]) * scale)
    return (grad_x, *outs)


def solution(mesh):
    dp = mesh.shape["dp"]
    mp = mesh.shape["mp"]
    sub = (dp // 8, 4, 2) if dp % 8 == 0 else (dp,)
    fine = Mesh(mesh.devices.reshape(*sub, mp), DP[-len(sub):] + ("mp",))
    names = DP[-len(sub):]
    in_specs = (
        P(names, "mp"),
        P(names, "mp"),
        P("mp", None, None),
        P("mp", None, None),
        P("mp", None, None),
        P("mp", None, None),
        P("mp", None, None),
        P("mp", None, None),
    )
    out_specs = (
        P(names, "mp"),
        P("mp", names, None),
        P("mp", names, None),
        P("mp", names, None),
        P("mp", names, None),
        P("mp", names, None),
        P("mp", names, None),
    )
    return jax.shard_map(shards, mesh=fine, in_specs=in_specs, out_specs=out_specs, check_vma=False)
```

```python
import math

import jax
import jax.numpy as jnp
from jax import lax
from jax.sharding import Mesh, PartitionSpec as P

BLK = 128
NBLK = 64
PAIR = 2
FBLK = 448
DP = ("dz", "dx", "dc")


def shards(tokens_in, grad_out, gate_in, gate_out, up_in, up_out, down_in, down_out):
    local_blocks = gate_in.shape[0]
    rows = tokens_in.shape[0]
    groups = lax.axis_size(DP)
    scale = 1.0 / math.sqrt(rows * groups)
    x_blocks = tokens_in.reshape(rows, local_blocks, BLK)
    dy_blocks = grad_out.reshape(rows, local_blocks, BLK)

    def mix_in(weight):
        shaped = weight.reshape(local_blocks, BLK, NBLK, PAIR)
        spread = jnp.einsum("tki,kijp->jkpt", x_blocks, shaped, preferred_element_type=jnp.float32)
        return spread.astype(jnp.bfloat16).reshape(NBLK, local_blocks * PAIR, rows)

    def widen(mixed, weight):
        return jnp.einsum("jct,jco->jot", mixed, weight, preferred_element_type=jnp.float32)

    gate_mid = mix_in(gate_in)
    up_mid = mix_in(up_in)
    back_shaped = down_out.reshape(local_blocks, NBLK, PAIR, BLK)
    back_mid = jnp.einsum(
        "tkr,kjpr->jkpt", dy_blocks, back_shaped, preferred_element_type=jnp.float32
    )
    back_mid = back_mid.astype(jnp.bfloat16).reshape(NBLK, local_blocks * PAIR, rows)
    first_recv = lax.all_to_all(
        jnp.stack([gate_mid, up_mid, back_mid]), "mp", split_axis=1, concat_axis=2, tiled=True
    )
    gate_recv, up_recv, back_recv = first_recv[0], first_recv[1], first_recv[2]
    gate_pre = widen(gate_recv, gate_out)
    up_pre = widen(up_recv, up_out)
    sigmoid_gate = jax.nn.sigmoid(gate_pre)
    activated = gate_pre * sigmoid_gate
    hidden = (activated * up_pre).astype(jnp.bfloat16)
    down_shaped = down_in.reshape(local_blocks, FBLK, NBLK, PAIR)
    down_mid = jnp.einsum("jot,jokp->kjpt", hidden, down_shaped, preferred_element_type=jnp.float32)
    down_mid = down_mid.astype(jnp.bfloat16).reshape(NBLK, local_blocks * PAIR, rows)
    down_recv = lax.all_to_all(down_mid, "mp", split_axis=0, concat_axis=1, tiled=True)
    term_down_out = jnp.einsum(
        "kct,tkr->kcr", down_recv, dy_blocks, preferred_element_type=jnp.float32
    )
    term_down_in = jnp.einsum("jot,jqt->joq", hidden, back_recv, preferred_element_type=jnp.float32)
    hidden_grad = jnp.einsum("joq,jqt->jot", down_in, back_recv, preferred_element_type=jnp.float32)
    gate_grad = (
        hidden_grad * up_pre * sigmoid_gate * (1.0 + gate_pre * (1.0 - sigmoid_gate))
    ).astype(jnp.bfloat16)
    up_grad = (hidden_grad * activated).astype(jnp.bfloat16)
    term_gate_out = jnp.einsum(
        "jct,jot->jco", gate_recv, gate_grad, preferred_element_type=jnp.float32
    )
    term_up_out = jnp.einsum("jct,jot->jco", up_recv, up_grad, preferred_element_type=jnp.float32)

    def narrow(grad, weight):
        shaped = weight.reshape(local_blocks, NBLK, PAIR, FBLK)
        spread = jnp.einsum("jot,jkpo->kjpt", grad, shaped, preferred_element_type=jnp.float32)
        return spread.astype(jnp.bfloat16).reshape(NBLK, local_blocks * PAIR, rows)

    back_recv2 = lax.all_to_all(
        jnp.stack([narrow(gate_grad, gate_out), narrow(up_grad, up_out)]),
        "mp", split_axis=1, concat_axis=2, tiled=True,
    )
    gate_back, up_back = back_recv2[0], back_recv2[1]
    input_grad = jnp.einsum("kio,kot->tki", gate_in, gate_back, preferred_element_type=jnp.float32)
    input_grad = input_grad + jnp.einsum(
        "kio,kot->tki", up_in, up_back, preferred_element_type=jnp.float32
    )
    term_gate_in = jnp.einsum(
        "tki,kot->kio", x_blocks, gate_back, preferred_element_type=jnp.float32
    )
    term_up_in = jnp.einsum("tki,kot->kio", x_blocks, up_back, preferred_element_type=jnp.float32)
    grad_x = input_grad.astype(jnp.bfloat16).reshape(rows, local_blocks * BLK)
    terms = (term_gate_in, term_gate_out, term_up_in, term_up_out, term_down_in, term_down_out)
    sizes = [lax.axis_size(name) for name in DP]

    def reduce_stage(summed, position, ring=False):
        wire = summed if position == len(DP) - 1 else summed.astype(jnp.bfloat16)
        if ring:
            return lax.psum_scatter(
                wire, DP[position], scatter_dimension=1 + position, tiled=True
            ).astype(jnp.float32)
        return lax.all_to_all(
            wire, DP[position], split_axis=1 + position, concat_axis=1 + position, tiled=True
        ).astype(jnp.float32).sum(axis=1 + position, keepdims=True)

    def inner_stages(members, ring):
        flat = [terms[m].reshape(terms[m].shape[0], groups, -1) for m in members]
        stacked = jnp.concatenate(flat, axis=2)
        summed = stacked.reshape(stacked.shape[0], *sizes, stacked.shape[2])
        for position in reversed(range(1, len(DP))):
            summed = reduce_stage(summed, position, ring)
        return summed, [piece.shape[2] for piece in flat]

    order = (1, 3, 4, 5, 0, 2)
    early, early_widths = inner_stages(order[:4], True)
    late, late_widths = inner_stages(order[4:], False)
    summed = reduce_stage(jnp.concatenate([early, late], axis=-1), 0)
    summed = summed.reshape(summed.shape[0], summed.shape[-1])
    outs = [None] * len(terms)
    start = 0
    for member, width in zip(order, early_widths + late_widths):
        term = terms[member]
        piece = summed[:, start:start + width]
        start += width
        outs[member] = piece.reshape(term.shape[0], term.shape[1] // groups, term.shape[2]) * scale
    return (grad_x, *outs)


def solution(mesh):
    dp = mesh.shape["dp"]
    mp = mesh.shape["mp"]
    sub = (dp // 8, 4, 2) if dp % 8 == 0 else (dp,)
    fine = Mesh(mesh.devices.reshape(*sub, mp), DP[-len(sub):] + ("mp",))
    names = DP[-len(sub):]
    in_specs = (
        P(names, "mp"),
        P(names, "mp"),
        P("mp", None, None),
        P("mp", None, None),
        P("mp", None, None),
        P("mp", None, None),
        P("mp", None, None),
        P("mp", None, None),
    )
    out_specs = (
        P(names, "mp"),
        P("mp", names, None),
        P("mp", names, None),
        P("mp", names, None),
        P("mp", names, None),
        P("mp", names, None),
        P("mp", names, None),
    )
    return jax.shard_map(shards, mesh=fine, in_specs=in_specs, out_specs=out_specs, check_vma=False)
```

```python
import math

import jax
import jax.numpy as jnp
from jax import lax
from jax.sharding import Mesh, PartitionSpec as P

BLK = 128
NBLK = 64
PAIR = 2
FBLK = 448
DP = ("dz", "dx", "dc")


def shards(tokens_in, grad_out, gate_in, gate_out, up_in, up_out, down_in, down_out):
    local_blocks = gate_in.shape[0]
    rows = tokens_in.shape[0]
    groups = lax.axis_size(DP)
    scale = 1.0 / math.sqrt(rows * groups)
    x_blocks = tokens_in.reshape(rows, local_blocks, BLK)
    dy_blocks = grad_out.reshape(rows, local_blocks, BLK)

    def mix_in(weight):
        shaped = weight.reshape(local_blocks, BLK, NBLK, PAIR)
        spread = jnp.einsum("tki,kijp->jkpt", x_blocks, shaped, preferred_element_type=jnp.float32)
        return spread.astype(jnp.bfloat16).reshape(NBLK, local_blocks * PAIR, rows)

    def widen(mixed, weight):
        return jnp.einsum("jct,jco->jot", mixed, weight, preferred_element_type=jnp.float32)

    gate_mid = mix_in(gate_in)
    up_mid = mix_in(up_in)
    back_shaped = down_out.reshape(local_blocks, NBLK, PAIR, BLK)
    back_mid = jnp.einsum(
        "tkr,kjpr->jkpt", dy_blocks, back_shaped, preferred_element_type=jnp.float32
    )
    back_mid = back_mid.astype(jnp.bfloat16).reshape(NBLK, local_blocks * PAIR, rows)
    first_recv = lax.all_to_all(
        jnp.stack([gate_mid, up_mid]), "mp", split_axis=1, concat_axis=2, tiled=True
    )
    gate_recv, up_recv = first_recv[0], first_recv[1]
    back_recv = lax.all_to_all(back_mid, "mp", split_axis=0, concat_axis=1, tiled=True)
    gate_pre = widen(gate_recv, gate_out)
    up_pre = widen(up_recv, up_out)
    sigmoid_gate = jax.nn.sigmoid(gate_pre)
    activated = gate_pre * sigmoid_gate
    hidden = (activated * up_pre).astype(jnp.bfloat16)
    down_shaped = down_in.reshape(local_blocks, FBLK, NBLK, PAIR)
    down_mid = jnp.einsum("jot,jokp->kjpt", hidden, down_shaped, preferred_element_type=jnp.float32)
    down_mid = down_mid.astype(jnp.bfloat16).reshape(NBLK, local_blocks * PAIR, rows)
    down_recv = lax.all_to_all(down_mid, "mp", split_axis=0, concat_axis=1, tiled=True)
    term_down_out = jnp.einsum(
        "kct,tkr->kcr", down_recv, dy_blocks, preferred_element_type=jnp.float32
    )
    term_down_in = jnp.einsum("jot,jqt->joq", hidden, back_recv, preferred_element_type=jnp.float32)
    hidden_grad = jnp.einsum("joq,jqt->jot", down_in, back_recv, preferred_element_type=jnp.float32)
    gate_grad = (
        hidden_grad * up_pre * sigmoid_gate * (1.0 + gate_pre * (1.0 - sigmoid_gate))
    ).astype(jnp.bfloat16)
    up_grad = (hidden_grad * activated).astype(jnp.bfloat16)
    term_gate_out = jnp.einsum(
        "jct,jot->jco", gate_recv, gate_grad, preferred_element_type=jnp.float32
    )
    term_up_out = jnp.einsum("jct,jot->jco", up_recv, up_grad, preferred_element_type=jnp.float32)

    def narrow(grad, weight):
        shaped = weight.reshape(local_blocks, NBLK, PAIR, FBLK)
        spread = jnp.einsum("jot,jkpo->kjpt", grad, shaped, preferred_element_type=jnp.float32)
        return spread.astype(jnp.bfloat16).reshape(NBLK, local_blocks * PAIR, rows)

    back_recv2 = lax.all_to_all(
        jnp.stack([narrow(gate_grad, gate_out), narrow(up_grad, up_out)]),
        "mp", split_axis=1, concat_axis=2, tiled=True,
    )
    gate_back, up_back = back_recv2[0], back_recv2[1]
    input_grad = jnp.einsum("kio,kot->tki", gate_in, gate_back, preferred_element_type=jnp.float32)
    input_grad = input_grad + jnp.einsum(
        "kio,kot->tki", up_in, up_back, preferred_element_type=jnp.float32
    )
    term_gate_in = jnp.einsum(
        "tki,kot->kio", x_blocks, gate_back, preferred_element_type=jnp.float32
    )
    term_up_in = jnp.einsum("tki,kot->kio", x_blocks, up_back, preferred_element_type=jnp.float32)
    grad_x = input_grad.astype(jnp.bfloat16).reshape(rows, local_blocks * BLK)
    terms = (term_gate_in, term_gate_out, term_up_in, term_up_out, term_down_in, term_down_out)
    flat = [term.reshape(term.shape[0], groups, -1) for term in terms]
    widths = [piece.shape[2] for piece in flat]
    stacked = jnp.concatenate(flat, axis=2)
    sizes = [lax.axis_size(name) for name in DP]
    summed = stacked.reshape(stacked.shape[0], *sizes, stacked.shape[2])
    for position in reversed(range(len(DP))):
        wire = summed.astype(jnp.bfloat16)
        summed = lax.all_to_all(
            wire, DP[position], split_axis=1 + position, concat_axis=1 + position, tiled=True
        ).astype(jnp.float32).sum(axis=1 + position, keepdims=True)
    summed = summed.reshape(stacked.shape[0], 1, stacked.shape[2])
    outs = []
    start = 0
    for term, width in zip(terms, widths):
        piece = summed[:, 0, start:start + width]
        start += width
        outs.append(piece.reshape(term.shape[0], term.shape[1] // groups, term.shape[2]) * scale)
    return (grad_x, *outs)


def solution(mesh):
    dp = mesh.shape["dp"]
    mp = mesh.shape["mp"]
    sub = (dp // 8, 4, 2) if dp % 8 == 0 else (dp,)
    fine = Mesh(mesh.devices.reshape(*sub, mp), DP[-len(sub):] + ("mp",))
    names = DP[-len(sub):]
    in_specs = (
        P(names, "mp"),
        P(names, "mp"),
        P("mp", None, None),
        P("mp", None, None),
        P("mp", None, None),
        P("mp", None, None),
        P("mp", None, None),
        P("mp", None, None),
    )
    out_specs = (
        P(names, "mp"),
        P("mp", names, None),
        P("mp", names, None),
        P("mp", names, None),
        P("mp", names, None),
        P("mp", names, None),
        P("mp", names, None),
    )
    return jax.shard_map(shards, mesh=fine, in_specs=in_specs, out_specs=out_specs, check_vma=False)
```

```python
import math

import jax
import jax.numpy as jnp
from jax import lax
from jax.sharding import Mesh, PartitionSpec as P

BLK = 128
NBLK = 64
PAIR = 2
FBLK = 448
DP = ("dz", "dx", "dc")


def shards(tokens_in, grad_out, gate_in, gate_out, up_in, up_out, down_in, down_out):
    local_blocks = gate_in.shape[0]
    rows = tokens_in.shape[0]
    groups = lax.axis_size(DP)
    scale = 1.0 / math.sqrt(rows * groups)
    x_blocks = tokens_in.reshape(rows, local_blocks, BLK)
    dy_blocks = grad_out.reshape(rows, local_blocks, BLK)

    def mix_in(weight):
        shaped = weight.reshape(local_blocks, BLK, NBLK, PAIR)
        spread = jnp.einsum("tki,kijp->jkpt", x_blocks, shaped, preferred_element_type=jnp.float32)
        return spread.astype(jnp.bfloat16).reshape(NBLK, local_blocks * PAIR, rows)

    def widen(mixed, weight):
        return jnp.einsum("jct,jco->jot", mixed, weight, preferred_element_type=jnp.float32)

    gate_mid = mix_in(gate_in)
    up_mid = mix_in(up_in)
    back_shaped = down_out.reshape(local_blocks, NBLK, PAIR, BLK)
    back_mid = jnp.einsum(
        "tkr,kjpr->jkpt", dy_blocks, back_shaped, preferred_element_type=jnp.float32
    )
    back_mid = back_mid.astype(jnp.bfloat16).reshape(NBLK, local_blocks * PAIR, rows)
    first_recv = lax.all_to_all(
        jnp.stack([gate_mid, up_mid, back_mid]), "mp", split_axis=1, concat_axis=2, tiled=True
    )
    gate_recv, up_recv, back_recv = first_recv[0], first_recv[1], first_recv[2]
    gate_pre = widen(gate_recv, gate_out)
    up_pre = widen(up_recv, up_out)
    sigmoid_gate = jax.nn.sigmoid(gate_pre)
    activated = gate_pre * sigmoid_gate
    hidden = (activated * up_pre).astype(jnp.bfloat16)
    down_shaped = down_in.reshape(local_blocks, FBLK, NBLK, PAIR)
    down_mid = jnp.einsum("jot,jokp->kjpt", hidden, down_shaped, preferred_element_type=jnp.float32)
    down_mid = down_mid.astype(jnp.bfloat16).reshape(NBLK, local_blocks * PAIR, rows)
    down_recv = lax.all_to_all(down_mid, "mp", split_axis=0, concat_axis=1, tiled=True)
    term_down_out = jnp.einsum(
        "kct,tkr->kcr", down_recv, dy_blocks, preferred_element_type=jnp.float32
    )
    term_down_in = jnp.einsum("jot,jqt->joq", hidden, back_recv, preferred_element_type=jnp.float32)
    hidden_grad = jnp.einsum("joq,jqt->jot", down_in, back_recv, preferred_element_type=jnp.float32)
    gate_grad = (
        hidden_grad * up_pre * sigmoid_gate * (1.0 + gate_pre * (1.0 - sigmoid_gate))
    ).astype(jnp.bfloat16)
    up_grad = (hidden_grad * activated).astype(jnp.bfloat16)
    term_gate_out = jnp.einsum(
        "jct,jot->jco", gate_recv, gate_grad, preferred_element_type=jnp.float32
    )
    term_up_out = jnp.einsum("jct,jot->jco", up_recv, up_grad, preferred_element_type=jnp.float32)

    def narrow(grad, weight):
        shaped = weight.reshape(local_blocks, NBLK, PAIR, FBLK)
        spread = jnp.einsum("jot,jkpo->kjpt", grad, shaped, preferred_element_type=jnp.float32)
        return spread.astype(jnp.bfloat16).reshape(NBLK, local_blocks * PAIR, rows)

    back_recv2 = lax.all_to_all(
        jnp.stack([narrow(gate_grad, gate_out), narrow(up_grad, up_out)]),
        "mp", split_axis=1, concat_axis=2, tiled=True,
    )
    gate_back, up_back = back_recv2[0], back_recv2[1]
    input_grad = jnp.einsum("kio,kot->tki", gate_in, gate_back, preferred_element_type=jnp.float32)
    input_grad = input_grad + jnp.einsum(
        "kio,kot->tki", up_in, up_back, preferred_element_type=jnp.float32
    )
    term_gate_in = jnp.einsum(
        "tki,kot->kio", x_blocks, gate_back, preferred_element_type=jnp.float32
    )
    term_up_in = jnp.einsum("tki,kot->kio", x_blocks, up_back, preferred_element_type=jnp.float32)
    grad_x = input_grad.astype(jnp.bfloat16).reshape(rows, local_blocks * BLK)
    terms = (term_gate_in, term_gate_out, term_up_in, term_up_out, term_down_in, term_down_out)
    flat = [(term * scale).reshape(term.shape[0], groups, -1) for term in terms]
    widths = [piece.shape[2] for piece in flat]
    stacked = jnp.concatenate(flat, axis=2)
    sizes = [lax.axis_size(name) for name in DP]
    summed = stacked.reshape(stacked.shape[0], *sizes, stacked.shape[2])
    for position in reversed(range(len(DP))):
        wire = summed if position == len(DP) - 1 else summed.astype(jnp.bfloat16)
        summed = lax.all_to_all(
            wire, DP[position], split_axis=1 + position, concat_axis=1 + position, tiled=True
        ).astype(jnp.float32).sum(axis=1 + position, keepdims=True)
    summed = summed.reshape(stacked.shape[0], 1, stacked.shape[2])
    outs = []
    start = 0
    for term, width in zip(terms, widths):
        piece = summed[:, 0, start:start + width]
        start += width
        outs.append(piece.reshape(term.shape[0], term.shape[1] // groups, term.shape[2]))
    return (grad_x, *outs)


def solution(mesh):
    dp = mesh.shape["dp"]
    mp = mesh.shape["mp"]
    sub = (dp // 8, 4, 2) if dp % 8 == 0 else (dp,)
    fine = Mesh(mesh.devices.reshape(*sub, mp), DP[-len(sub):] + ("mp",))
    names = DP[-len(sub):]
    in_specs = (
        P(names, "mp"),
        P(names, "mp"),
        P("mp", None, None),
        P("mp", None, None),
        P("mp", None, None),
        P("mp", None, None),
        P("mp", None, None),
        P("mp", None, None),
    )
    out_specs = (
        P(names, "mp"),
        P("mp", names, None),
        P("mp", names, None),
        P("mp", names, None),
        P("mp", names, None),
        P("mp", names, None),
        P("mp", names, None),
    )
    return jax.shard_map(shards, mesh=fine, in_specs=in_specs, out_specs=out_specs, check_vma=False)
```

```python
import math

import jax
import jax.numpy as jnp
from jax import lax
from jax.sharding import Mesh, PartitionSpec as P

BLK = 128
NBLK = 64
PAIR = 2
FBLK = 448
DP = ("dz", "dx", "dc")


def ring_scatter(summed, name, dim):
    count = lax.axis_size(name)
    me = lax.axis_index(name)
    half = summed.shape[-1] // 2
    ahead, behind = summed[..., :half], summed[..., half:]
    clockwise = [(j, (j + 1) % count) for j in range(count)]
    counter = [(j, (j - 1) % count) for j in range(count)]

    def take(values, shift):
        return lax.dynamic_index_in_dim(values, (me + 2 * count + shift) % count, axis=dim)

    carry_a, carry_b = take(ahead, -1), take(behind, 1)
    for step in range(count - 1):
        got_a = lax.ppermute(carry_a.astype(jnp.bfloat16), name, clockwise).astype(jnp.float32)
        got_b = lax.ppermute(carry_b.astype(jnp.bfloat16), name, counter).astype(jnp.float32)
        carry_a = got_a + take(ahead, -step - 2)
        carry_b = got_b + take(behind, step + 2)
    return jnp.concatenate([carry_a, carry_b], axis=-1)


def shards(tokens_in, grad_out, gate_in, gate_out, up_in, up_out, down_in, down_out):
    local_blocks = gate_in.shape[0]
    rows = tokens_in.shape[0]
    groups = lax.axis_size(DP)
    scale = 1.0 / math.sqrt(rows * groups)
    x_blocks = tokens_in.reshape(rows, local_blocks, BLK)
    dy_blocks = grad_out.reshape(rows, local_blocks, BLK)

    def mix_in(weight):
        shaped = weight.reshape(local_blocks, BLK, NBLK, PAIR)
        spread = jnp.einsum("tki,kijp->jkpt", x_blocks, shaped, preferred_element_type=jnp.float32)
        return spread.astype(jnp.bfloat16).reshape(NBLK, local_blocks * PAIR, rows)

    def widen(mixed, weight):
        return jnp.einsum("jct,jco->jot", mixed, weight, preferred_element_type=jnp.float32)

    gate_mid = mix_in(gate_in)
    up_mid = mix_in(up_in)
    back_shaped = down_out.reshape(local_blocks, NBLK, PAIR, BLK)
    back_mid = jnp.einsum(
        "tkr,kjpr->jkpt", dy_blocks, back_shaped, preferred_element_type=jnp.float32
    )
    back_mid = back_mid.astype(jnp.bfloat16).reshape(NBLK, local_blocks * PAIR, rows)
    first_recv = lax.all_to_all(
        jnp.stack([gate_mid, up_mid, back_mid]), "mp", split_axis=1, concat_axis=2, tiled=True
    )
    gate_recv, up_recv, back_recv = first_recv[0], first_recv[1], first_recv[2]
    gate_pre = widen(gate_recv, gate_out)
    up_pre = widen(up_recv, up_out)
    sigmoid_gate = jax.nn.sigmoid(gate_pre)
    activated = gate_pre * sigmoid_gate
    hidden = (activated * up_pre).astype(jnp.bfloat16)
    down_shaped = down_in.reshape(local_blocks, FBLK, NBLK, PAIR)
    down_mid = jnp.einsum("jot,jokp->kjpt", hidden, down_shaped, preferred_element_type=jnp.float32)
    down_mid = down_mid.astype(jnp.bfloat16).reshape(NBLK, local_blocks * PAIR, rows)
    down_recv = lax.all_to_all(down_mid, "mp", split_axis=0, concat_axis=1, tiled=True)
    term_down_out = jnp.einsum(
        "kct,tkr->kcr", down_recv, dy_blocks, preferred_element_type=jnp.float32
    )
    term_down_in = jnp.einsum("jot,jqt->joq", hidden, back_recv, preferred_element_type=jnp.float32)
    hidden_grad = jnp.einsum("joq,jqt->jot", down_in, back_recv, preferred_element_type=jnp.float32)
    gate_grad = (
        hidden_grad * up_pre * sigmoid_gate * (1.0 + gate_pre * (1.0 - sigmoid_gate))
    ).astype(jnp.bfloat16)
    up_grad = (hidden_grad * activated).astype(jnp.bfloat16)
    term_gate_out = jnp.einsum(
        "jct,jot->jco", gate_recv, gate_grad, preferred_element_type=jnp.float32
    )
    term_up_out = jnp.einsum("jct,jot->jco", up_recv, up_grad, preferred_element_type=jnp.float32)

    def narrow(grad, weight):
        shaped = weight.reshape(local_blocks, NBLK, PAIR, FBLK)
        spread = jnp.einsum("jot,jkpo->kjpt", grad, shaped, preferred_element_type=jnp.float32)
        return spread.astype(jnp.bfloat16).reshape(NBLK, local_blocks * PAIR, rows)

    back_recv2 = lax.all_to_all(
        jnp.stack([narrow(gate_grad, gate_out), narrow(up_grad, up_out)]),
        "mp", split_axis=1, concat_axis=2, tiled=True,
    )
    gate_back, up_back = back_recv2[0], back_recv2[1]
    input_grad = jnp.einsum("kio,kot->tki", gate_in, gate_back, preferred_element_type=jnp.float32)
    input_grad = input_grad + jnp.einsum(
        "kio,kot->tki", up_in, up_back, preferred_element_type=jnp.float32
    )
    term_gate_in = jnp.einsum(
        "tki,kot->kio", x_blocks, gate_back, preferred_element_type=jnp.float32
    )
    term_up_in = jnp.einsum("tki,kot->kio", x_blocks, up_back, preferred_element_type=jnp.float32)
    grad_x = input_grad.astype(jnp.bfloat16).reshape(rows, local_blocks * BLK)
    terms = (term_gate_in, term_gate_out, term_up_in, term_up_out, term_down_in, term_down_out)
    flat = [term.reshape(term.shape[0], groups, -1) for term in terms]
    widths = [piece.shape[2] for piece in flat]
    stacked = jnp.concatenate(flat, axis=2)
    sizes = [lax.axis_size(name) for name in DP]
    summed = stacked.reshape(stacked.shape[0], *sizes, stacked.shape[2])
    for position in reversed(range(len(DP))):
        if position == 1:
            summed = ring_scatter(summed, DP[position], 1 + position)
            continue
        wire = summed if position == len(DP) - 1 else summed.astype(jnp.bfloat16)
        summed = lax.all_to_all(
            wire, DP[position], split_axis=1 + position, concat_axis=1 + position, tiled=True
        ).astype(jnp.float32).sum(axis=1 + position, keepdims=True)
    summed = summed.reshape(stacked.shape[0], 1, stacked.shape[2])
    outs = []
    start = 0
    for term, width in zip(terms, widths):
        piece = summed[:, 0, start:start + width]
        start += width
        outs.append(piece.reshape(term.shape[0], term.shape[1] // groups, term.shape[2]) * scale)
    return (grad_x, *outs)


def solution(mesh):
    dp = mesh.shape["dp"]
    mp = mesh.shape["mp"]
    sub = (dp // 8, 4, 2) if dp % 8 == 0 else (dp,)
    fine = Mesh(mesh.devices.reshape(*sub, mp), DP[-len(sub):] + ("mp",))
    names = DP[-len(sub):]
    in_specs = (
        P(names, "mp"),
        P(names, "mp"),
        P("mp", None, None),
        P("mp", None, None),
        P("mp", None, None),
        P("mp", None, None),
        P("mp", None, None),
        P("mp", None, None),
    )
    out_specs = (
        P(names, "mp"),
        P("mp", names, None),
        P("mp", names, None),
        P("mp", names, None),
        P("mp", names, None),
        P("mp", names, None),
        P("mp", names, None),
    )
    return jax.shard_map(shards, mesh=fine, in_specs=in_specs, out_specs=out_specs, check_vma=False)
```

```python
import math

import jax
import jax.numpy as jnp
from jax import lax
from jax.sharding import Mesh, PartitionSpec as P

BLK = 128
NBLK = 64
PAIR = 2
FBLK = 448
DP = ("dz", "dx", "dc")


def shards(tokens_in, grad_out, gate_in, gate_out, up_in, up_out, down_in, down_out):
    local_blocks = gate_in.shape[0]
    rows = tokens_in.shape[0]
    groups = lax.axis_size(DP)
    scale = 1.0 / math.sqrt(rows * groups)
    x_blocks = tokens_in.reshape(rows, local_blocks, BLK)
    dy_blocks = grad_out.reshape(rows, local_blocks, BLK)

    def mix_in(weight):
        shaped = weight.reshape(local_blocks, BLK, NBLK, PAIR)
        spread = jnp.einsum("tki,kijp->jkpt", x_blocks, shaped, preferred_element_type=jnp.float32)
        return spread.astype(jnp.bfloat16).reshape(NBLK, local_blocks * PAIR, rows)

    def widen(mixed, weight):
        return jnp.einsum("jct,jco->jot", mixed, weight, preferred_element_type=jnp.float32)

    gate_mid = mix_in(gate_in)
    up_mid = mix_in(up_in)
    back_shaped = down_out.reshape(local_blocks, NBLK, PAIR, BLK)
    back_mid = jnp.einsum(
        "tkr,kjpr->jkpt", dy_blocks, back_shaped, preferred_element_type=jnp.float32
    )
    back_mid = back_mid.astype(jnp.bfloat16).reshape(NBLK, local_blocks * PAIR, rows)
    first_recv = lax.all_to_all(
        jnp.stack([gate_mid, up_mid, back_mid]), "mp", split_axis=1, concat_axis=2, tiled=True
    )
    gate_recv, up_recv, back_recv = first_recv[0], first_recv[1], first_recv[2]
    gate_pre = widen(gate_recv, gate_out)
    up_pre = widen(up_recv, up_out)
    sigmoid_gate = jax.nn.sigmoid(gate_pre)
    activated = gate_pre * sigmoid_gate
    hidden = (activated * up_pre).astype(jnp.bfloat16)
    down_shaped = down_in.reshape(local_blocks, FBLK, NBLK, PAIR)
    down_mid = jnp.einsum("jot,jokp->kjpt", hidden, down_shaped, preferred_element_type=jnp.float32)
    down_mid = down_mid.astype(jnp.bfloat16).reshape(NBLK, local_blocks * PAIR, rows)
    down_recv = lax.all_to_all(down_mid, "mp", split_axis=0, concat_axis=1, tiled=True)
    term_down_out = jnp.einsum(
        "kct,tkr->kcr", down_recv, dy_blocks, preferred_element_type=jnp.float32
    )
    term_down_in = jnp.einsum("jot,jqt->joq", hidden, back_recv, preferred_element_type=jnp.float32)
    hidden_grad = jnp.einsum("joq,jqt->jot", down_in, back_recv, preferred_element_type=jnp.float32)
    gate_grad = (
        hidden_grad * up_pre * sigmoid_gate * (1.0 + gate_pre * (1.0 - sigmoid_gate))
    ).astype(jnp.bfloat16)
    up_grad = (hidden_grad * activated).astype(jnp.bfloat16)
    term_gate_out = jnp.einsum(
        "jct,jot->jco", gate_recv, gate_grad, preferred_element_type=jnp.float32
    )
    term_up_out = jnp.einsum("jct,jot->jco", up_recv, up_grad, preferred_element_type=jnp.float32)

    def narrow(grad, weight):
        shaped = weight.reshape(local_blocks, NBLK, PAIR, FBLK)
        spread = jnp.einsum("jot,jkpo->kjpt", grad, shaped, preferred_element_type=jnp.float32)
        return spread.astype(jnp.bfloat16).reshape(NBLK, local_blocks * PAIR, rows)

    back_recv2 = lax.all_to_all(
        jnp.stack([narrow(gate_grad, gate_out), narrow(up_grad, up_out)]),
        "mp", split_axis=1, concat_axis=2, tiled=True,
    )
    gate_back, up_back = back_recv2[0], back_recv2[1]
    term_gate_in = jnp.einsum(
        "tki,kot->kio", x_blocks, gate_back, preferred_element_type=jnp.float32
    )
    term_up_in = jnp.einsum("tki,kot->kio", x_blocks, up_back, preferred_element_type=jnp.float32)
    terms = (term_gate_in, term_gate_out, term_up_in, term_up_out, term_down_in, term_down_out)
    flat = [term.reshape(term.shape[0], groups, -1) for term in terms]
    widths = [piece.shape[2] for piece in flat]
    stacked = jnp.concatenate(flat, axis=2)
    sizes = [lax.axis_size(name) for name in DP]
    summed = stacked.reshape(stacked.shape[0], *sizes, stacked.shape[2])
    for position in reversed(range(len(DP))):
        wire = summed if position == len(DP) - 1 else summed.astype(jnp.bfloat16)
        if position == 0:
            wire, gate_back, up_back = lax.optimization_barrier((wire, gate_back, up_back))
        summed = lax.all_to_all(
            wire, DP[position], split_axis=1 + position, concat_axis=1 + position, tiled=True
        ).astype(jnp.float32).sum(axis=1 + position, keepdims=True)
    summed = summed.reshape(stacked.shape[0], 1, stacked.shape[2])
    outs = []
    start = 0
    for term, width in zip(terms, widths):
        piece = summed[:, 0, start:start + width]
        start += width
        outs.append(piece.reshape(term.shape[0], term.shape[1] // groups, term.shape[2]) * scale)
    input_grad = jnp.einsum("kio,kot->tki", gate_in, gate_back, preferred_element_type=jnp.float32)
    input_grad = input_grad + jnp.einsum(
        "kio,kot->tki", up_in, up_back, preferred_element_type=jnp.float32
    )
    grad_x = input_grad.astype(jnp.bfloat16).reshape(rows, local_blocks * BLK)
    return (grad_x, *outs)


def solution(mesh):
    dp = mesh.shape["dp"]
    mp = mesh.shape["mp"]
    sub = (dp // 8, 4, 2) if dp % 8 == 0 else (dp,)
    fine = Mesh(mesh.devices.reshape(*sub, mp), DP[-len(sub):] + ("mp",))
    names = DP[-len(sub):]
    in_specs = (
        P(names, "mp"),
        P(names, "mp"),
        P("mp", None, None),
        P("mp", None, None),
        P("mp", None, None),
        P("mp", None, None),
        P("mp", None, None),
        P("mp", None, None),
    )
    out_specs = (
        P(names, "mp"),
        P("mp", names, None),
        P("mp", names, None),
        P("mp", names, None),
        P("mp", names, None),
        P("mp", names, None),
        P("mp", names, None),
    )
    return jax.shard_map(shards, mesh=fine, in_specs=in_specs, out_specs=out_specs, check_vma=False)
```

```python
import math

import jax
import jax.numpy as jnp
from jax import lax
from jax.sharding import Mesh, PartitionSpec as P

BLK = 128
NBLK = 64
PAIR = 2
FBLK = 448
DP = ("dz", "dx", "dc")


def shards(tokens_in, grad_out, gate_in, gate_out, up_in, up_out, down_in, down_out):
    local_blocks = gate_in.shape[0]
    rows = tokens_in.shape[0]
    groups = lax.axis_size(DP)
    scale = 1.0 / math.sqrt(rows * groups)
    x_blocks = tokens_in.reshape(rows, local_blocks, BLK)
    dy_blocks = grad_out.reshape(rows, local_blocks, BLK)

    def mix_in(weight):
        shaped = weight.reshape(local_blocks, BLK, NBLK, PAIR)
        spread = jnp.einsum("tki,kijp->jkpt", x_blocks, shaped, preferred_element_type=jnp.float32)
        return spread.astype(jnp.bfloat16).reshape(NBLK, local_blocks * PAIR, rows)

    def widen(mixed, weight):
        return jnp.einsum("jct,jco->jot", mixed, weight, preferred_element_type=jnp.float32)

    gate_mid = mix_in(gate_in)
    up_mid = mix_in(up_in)
    back_shaped = down_out.reshape(local_blocks, NBLK, PAIR, BLK)
    back_mid = jnp.einsum(
        "tkr,kjpr->jkpt", dy_blocks, back_shaped, preferred_element_type=jnp.float32
    )
    back_mid = back_mid.astype(jnp.bfloat16).reshape(NBLK, local_blocks * PAIR, rows)
    first_recv = lax.all_to_all(
        jnp.stack([gate_mid, up_mid, back_mid]), "mp", split_axis=1, concat_axis=2, tiled=True
    )
    gate_recv, up_recv, back_recv = first_recv[0], first_recv[1], first_recv[2]
    gate_pre = widen(gate_recv, gate_out)
    up_pre = widen(up_recv, up_out)
    sigmoid_gate = jax.nn.sigmoid(gate_pre)
    activated = gate_pre * sigmoid_gate
    hidden = (activated * up_pre).astype(jnp.bfloat16)
    down_shaped = down_in.reshape(local_blocks, FBLK, NBLK, PAIR)
    down_mid = jnp.einsum("jot,jokp->kjpt", hidden, down_shaped, preferred_element_type=jnp.float32)
    down_mid = down_mid.astype(jnp.bfloat16).reshape(NBLK, local_blocks * PAIR, rows)
    down_recv = lax.all_to_all(down_mid, "mp", split_axis=0, concat_axis=1, tiled=True)
    term_down_out = jnp.einsum(
        "kct,tkr->kcr", down_recv, dy_blocks, preferred_element_type=jnp.float32
    )
    term_down_in = jnp.einsum("jot,jqt->joq", hidden, back_recv, preferred_element_type=jnp.float32)
    hidden_grad = jnp.einsum("joq,jqt->jot", down_in, back_recv, preferred_element_type=jnp.float32)
    gate_grad = (
        hidden_grad * up_pre * sigmoid_gate * (1.0 + gate_pre * (1.0 - sigmoid_gate))
    ).astype(jnp.bfloat16)
    up_grad = (hidden_grad * activated).astype(jnp.bfloat16)
    term_gate_out = jnp.einsum(
        "jct,jot->jco", gate_recv, gate_grad, preferred_element_type=jnp.float32
    )
    term_up_out = jnp.einsum("jct,jot->jco", up_recv, up_grad, preferred_element_type=jnp.float32)

    def narrow(grad, weight):
        shaped = weight.reshape(local_blocks, NBLK, PAIR, FBLK)
        spread = jnp.einsum("jot,jkpo->kjpt", grad, shaped, preferred_element_type=jnp.float32)
        return spread.astype(jnp.bfloat16).reshape(NBLK, local_blocks * PAIR, rows)

    back_recv2 = lax.all_to_all(
        jnp.stack([narrow(gate_grad, gate_out), narrow(up_grad, up_out)]),
        "mp", split_axis=1, concat_axis=2, tiled=True,
    )
    gate_back, up_back = back_recv2[0], back_recv2[1]
    input_grad = jnp.einsum("kio,kot->tki", gate_in, gate_back, preferred_element_type=jnp.float32)
    input_grad = input_grad + jnp.einsum(
        "kio,kot->tki", up_in, up_back, preferred_element_type=jnp.float32
    )
    term_gate_in = jnp.einsum(
        "tki,kot->kio", x_blocks, gate_back, preferred_element_type=jnp.float32
    )
    term_up_in = jnp.einsum("tki,kot->kio", x_blocks, up_back, preferred_element_type=jnp.float32)
    grad_x = input_grad.astype(jnp.bfloat16).reshape(rows, local_blocks * BLK)
    terms = (term_gate_in, term_gate_out, term_up_in, term_up_out, term_down_in, term_down_out)
    flat = [term.reshape(term.shape[0], groups, -1) for term in terms]
    widths = [piece.shape[2] for piece in flat]
    stacked = jnp.concatenate(flat, axis=2)
    sizes = [lax.axis_size(name) for name in DP]
    summed = stacked.reshape(stacked.shape[0], *sizes, stacked.shape[2])
    for position in reversed(range(len(DP))):
        if position == len(DP) - 1 and sizes[position] == 2:
            me = lax.axis_index(DP[position])
            own = lax.dynamic_index_in_dim(summed, me, axis=1 + position)
            other = lax.dynamic_index_in_dim(summed, 1 - me, axis=1 + position)
            summed = own + lax.ppermute(other, DP[position], [(0, 1), (1, 0)])
            continue
        wire = summed if position == len(DP) - 1 else summed.astype(jnp.bfloat16)
        summed = lax.all_to_all(
            wire, DP[position], split_axis=1 + position, concat_axis=1 + position, tiled=True
        ).astype(jnp.float32).sum(axis=1 + position, keepdims=True)
    summed = summed.reshape(stacked.shape[0], 1, stacked.shape[2])
    outs = []
    start = 0
    for term, width in zip(terms, widths):
        piece = summed[:, 0, start:start + width]
        start += width
        outs.append(piece.reshape(term.shape[0], term.shape[1] // groups, term.shape[2]) * scale)
    return (grad_x, *outs)


def solution(mesh):
    dp = mesh.shape["dp"]
    mp = mesh.shape["mp"]
    sub = (dp // 8, 4, 2) if dp % 8 == 0 else (dp,)
    fine = Mesh(mesh.devices.reshape(*sub, mp), DP[-len(sub):] + ("mp",))
    names = DP[-len(sub):]
    in_specs = (
        P(names, "mp"),
        P(names, "mp"),
        P("mp", None, None),
        P("mp", None, None),
        P("mp", None, None),
        P("mp", None, None),
        P("mp", None, None),
        P("mp", None, None),
    )
    out_specs = (
        P(names, "mp"),
        P("mp", names, None),
        P("mp", names, None),
        P("mp", names, None),
        P("mp", names, None),
        P("mp", names, None),
        P("mp", names, None),
    )
    return jax.shard_map(shards, mesh=fine, in_specs=in_specs, out_specs=out_specs, check_vma=False)
```

```python
import math

import jax
import jax.numpy as jnp
from jax import lax
from jax.sharding import Mesh, PartitionSpec as P

BLK = 128
NBLK = 64
PAIR = 2
FBLK = 448
DP = ("dz", "dx", "dc")


def shards(tokens_in, grad_out, gate_in, gate_out, up_in, up_out, down_in, down_out):
    local_blocks = gate_in.shape[0]
    rows = tokens_in.shape[0]
    groups = lax.axis_size(DP)
    scale = 1.0 / math.sqrt(rows * groups)
    x_blocks = tokens_in.reshape(rows, local_blocks, BLK)
    dy_blocks = grad_out.reshape(rows, local_blocks, BLK)

    def mix_in(weight):
        shaped = weight.reshape(local_blocks, BLK, NBLK, PAIR)
        spread = jnp.einsum("tki,kijp->jkpt", x_blocks, shaped, preferred_element_type=jnp.float32)
        return spread.astype(jnp.bfloat16).reshape(NBLK, local_blocks * PAIR, rows)

    def widen(mixed, weight):
        return jnp.einsum("jct,jco->jot", mixed, weight, preferred_element_type=jnp.float32)

    gate_mid = mix_in(gate_in)
    up_mid = mix_in(up_in)
    back_shaped = down_out.reshape(local_blocks, NBLK, PAIR, BLK)
    back_mid = jnp.einsum(
        "tkr,kjpr->jkpt", dy_blocks, back_shaped, preferred_element_type=jnp.float32
    )
    back_mid = back_mid.astype(jnp.bfloat16).reshape(NBLK, local_blocks * PAIR, rows)
    first_recv = lax.all_to_all(
        jnp.stack([gate_mid, up_mid, back_mid]), "mp", split_axis=1, concat_axis=2, tiled=True
    )
    gate_recv, up_recv, back_recv = first_recv[0], first_recv[1], first_recv[2]
    gate_pre = widen(gate_recv, gate_out)
    up_pre = widen(up_recv, up_out)
    sigmoid_gate = jax.nn.sigmoid(gate_pre)
    activated = gate_pre * sigmoid_gate
    hidden = (activated * up_pre).astype(jnp.bfloat16)
    down_shaped = down_in.reshape(local_blocks, FBLK, NBLK, PAIR)
    down_mid = jnp.einsum("jot,jokp->kjpt", hidden, down_shaped, preferred_element_type=jnp.float32)
    down_mid = down_mid.astype(jnp.bfloat16).reshape(NBLK, local_blocks * PAIR, rows)
    down_recv = lax.all_to_all(down_mid, "mp", split_axis=0, concat_axis=1, tiled=True)
    term_down_out = jnp.einsum(
        "kct,tkr->kcr", down_recv, dy_blocks, preferred_element_type=jnp.float32
    )
    term_down_in = jnp.einsum("jot,jqt->joq", hidden, back_recv, preferred_element_type=jnp.float32)
    hidden_grad = jnp.einsum("joq,jqt->jot", down_in, back_recv, preferred_element_type=jnp.float32)
    gate_grad = (
        hidden_grad * up_pre * sigmoid_gate * (1.0 + gate_pre * (1.0 - sigmoid_gate))
    ).astype(jnp.bfloat16)
    up_grad = (hidden_grad * activated).astype(jnp.bfloat16)
    term_gate_out = jnp.einsum(
        "jct,jot->jco", gate_recv, gate_grad, preferred_element_type=jnp.float32
    )
    term_up_out = jnp.einsum("jct,jot->jco", up_recv, up_grad, preferred_element_type=jnp.float32)

    def narrow(grad, weight):
        shaped = weight.reshape(local_blocks, NBLK, PAIR, FBLK)
        spread = jnp.einsum("jot,jkpo->kjpt", grad, shaped, preferred_element_type=jnp.float32)
        return spread.astype(jnp.bfloat16).reshape(NBLK, local_blocks * PAIR, rows)

    back_recv2 = lax.all_to_all(
        jnp.stack([narrow(gate_grad, gate_out), narrow(up_grad, up_out)]),
        "mp", split_axis=1, concat_axis=2, tiled=True,
    )
    gate_back, up_back = back_recv2[0], back_recv2[1]
    input_grad = jnp.einsum("kio,kot->tki", gate_in, gate_back, preferred_element_type=jnp.float32)
    input_grad = input_grad + jnp.einsum(
        "kio,kot->tki", up_in, up_back, preferred_element_type=jnp.float32
    )
    term_gate_in = jnp.einsum(
        "tki,kot->kio", x_blocks, gate_back, preferred_element_type=jnp.float32
    )
    term_up_in = jnp.einsum("tki,kot->kio", x_blocks, up_back, preferred_element_type=jnp.float32)
    grad_x = input_grad.astype(jnp.bfloat16).reshape(rows, local_blocks * BLK)
    terms = (term_gate_in, term_gate_out, term_up_in, term_up_out, term_down_in, term_down_out)
    sizes = [lax.axis_size(name) for name in DP]
    me = lax.axis_index(DP[-1])

    def pair_stage(members):
        flat = [terms[m].reshape(terms[m].shape[0], groups, -1) for m in members]
        stacked = jnp.concatenate(flat, axis=2)
        summed = stacked.reshape(stacked.shape[0], *sizes, stacked.shape[2])
        own = lax.dynamic_index_in_dim(summed, me, axis=len(DP), keepdims=False)
        other = lax.dynamic_index_in_dim(summed, 1 - me, axis=len(DP), keepdims=False)
        return own + lax.ppermute(other, DP[-1], [(0, 1), (1, 0)]), [p.shape[2] for p in flat]

    order = (1, 3, 4, 5, 0, 2)
    early, early_widths = pair_stage(order[:4])
    late, late_widths = pair_stage(order[4:])
    summed = jnp.expand_dims(jnp.concatenate([early, late], axis=-1), len(DP))
    for position in reversed(range(len(DP) - 1)):
        summed = lax.all_to_all(
            summed.astype(jnp.bfloat16), DP[position], split_axis=1 + position,
            concat_axis=1 + position, tiled=True,
        ).astype(jnp.float32).sum(axis=1 + position, keepdims=True)
    summed = summed.reshape(summed.shape[0], summed.shape[-1])
    outs = [None] * len(terms)
    start = 0
    for member, width in zip(order, early_widths + late_widths):
        term = terms[member]
        piece = summed[:, start:start + width]
        start += width
        outs[member] = piece.reshape(term.shape[0], term.shape[1] // groups, term.shape[2]) * scale
    return (grad_x, *outs)


def solution(mesh):
    dp = mesh.shape["dp"]
    mp = mesh.shape["mp"]
    sub = (dp // 8, 4, 2) if dp % 8 == 0 else (dp,)
    fine = Mesh(mesh.devices.reshape(*sub, mp), DP[-len(sub):] + ("mp",))
    names = DP[-len(sub):]
    in_specs = (
        P(names, "mp"),
        P(names, "mp"),
        P("mp", None, None),
        P("mp", None, None),
        P("mp", None, None),
        P("mp", None, None),
        P("mp", None, None),
        P("mp", None, None),
    )
    out_specs = (
        P(names, "mp"),
        P("mp", names, None),
        P("mp", names, None),
        P("mp", names, None),
        P("mp", names, None),
        P("mp", names, None),
        P("mp", names, None),
    )
    return jax.shard_map(shards, mesh=fine, in_specs=in_specs, out_specs=out_specs, check_vma=False)
```

```python
import math

import jax
import jax.numpy as jnp
from jax import lax
from jax.sharding import Mesh, PartitionSpec as P

BLK = 128
NBLK = 64
PAIR = 2
FBLK = 448
DP = ("dz", "dx", "dc")


def shards(tokens_in, grad_out, gate_in, gate_out, up_in, up_out, down_in, down_out):
    local_blocks = gate_in.shape[0]
    rows = tokens_in.shape[0]
    groups = lax.axis_size(DP)
    scale = 1.0 / math.sqrt(rows * groups)
    x_blocks = tokens_in.reshape(rows, local_blocks, BLK)
    dy_blocks = grad_out.reshape(rows, local_blocks, BLK)

    def mix_in(weight):
        shaped = weight.reshape(local_blocks, BLK, NBLK, PAIR)
        spread = jnp.einsum("tki,kijp->jkpt", x_blocks, shaped, preferred_element_type=jnp.float32)
        return spread.astype(jnp.bfloat16).reshape(NBLK, local_blocks * PAIR, rows)

    def widen(mixed, weight):
        return jnp.einsum("jct,jco->jot", mixed, weight, preferred_element_type=jnp.float32)

    gate_mid = mix_in(gate_in)
    up_mid = mix_in(up_in)
    back_shaped = down_out.reshape(local_blocks, NBLK, PAIR, BLK)
    back_mid = jnp.einsum(
        "tkr,kjpr->jkpt", dy_blocks, back_shaped, preferred_element_type=jnp.float32
    )
    back_mid = back_mid.astype(jnp.bfloat16).reshape(NBLK, local_blocks * PAIR, rows)
    first_recv = lax.all_to_all(
        jnp.stack([gate_mid, up_mid, back_mid]), "mp", split_axis=1, concat_axis=2, tiled=True
    )
    gate_recv, up_recv, back_recv = first_recv[0], first_recv[1], first_recv[2]
    gate_pre = widen(gate_recv, gate_out)
    up_pre = widen(up_recv, up_out)
    sigmoid_gate = jax.nn.sigmoid(gate_pre)
    activated = gate_pre * sigmoid_gate
    hidden = (activated * up_pre).astype(jnp.bfloat16)
    down_shaped = down_in.reshape(local_blocks, FBLK, NBLK, PAIR)
    down_mid = jnp.einsum("jot,jokp->kjpt", hidden, down_shaped, preferred_element_type=jnp.float32)
    down_mid = down_mid.astype(jnp.bfloat16).reshape(NBLK, local_blocks * PAIR, rows)
    down_recv = lax.all_to_all(down_mid, "mp", split_axis=0, concat_axis=1, tiled=True)
    term_down_out = jnp.einsum(
        "kct,tkr->kcr", down_recv, dy_blocks, preferred_element_type=jnp.float32
    )
    term_down_in = jnp.einsum("jot,jqt->joq", hidden, back_recv, preferred_element_type=jnp.float32)
    hidden_grad = jnp.einsum("joq,jqt->jot", down_in, back_recv, preferred_element_type=jnp.float32)
    gate_grad = (
        hidden_grad * up_pre * sigmoid_gate * (1.0 + gate_pre * (1.0 - sigmoid_gate))
    ).astype(jnp.bfloat16)
    up_grad = (hidden_grad * activated).astype(jnp.bfloat16)
    term_gate_out = jnp.einsum(
        "jct,jot->jco", gate_recv, gate_grad, preferred_element_type=jnp.float32
    )
    term_up_out = jnp.einsum("jct,jot->jco", up_recv, up_grad, preferred_element_type=jnp.float32)

    def narrow(grad, weight):
        shaped = weight.reshape(local_blocks, NBLK, PAIR, FBLK)
        spread = jnp.einsum("jot,jkpo->kjpt", grad, shaped, preferred_element_type=jnp.float32)
        return spread.astype(jnp.bfloat16).reshape(NBLK, local_blocks * PAIR, rows)

    back_recv2 = lax.all_to_all(
        jnp.stack([narrow(gate_grad, gate_out), narrow(up_grad, up_out)]),
        "mp", split_axis=1, concat_axis=2, tiled=True,
    )
    gate_back, up_back = back_recv2[0], back_recv2[1]
    input_grad = jnp.einsum("kio,kot->tki", gate_in, gate_back, preferred_element_type=jnp.float32)
    input_grad = input_grad + jnp.einsum(
        "kio,kot->tki", up_in, up_back, preferred_element_type=jnp.float32
    )
    term_gate_in = jnp.einsum(
        "tki,kot->kio", x_blocks, gate_back, preferred_element_type=jnp.float32
    )
    term_up_in = jnp.einsum("tki,kot->kio", x_blocks, up_back, preferred_element_type=jnp.float32)
    grad_x = input_grad.astype(jnp.bfloat16).reshape(rows, local_blocks * BLK)
    terms = (term_gate_in, term_gate_out, term_up_in, term_up_out, term_down_in, term_down_out)
    flat = [term.reshape(term.shape[0], groups, -1) for term in terms]
    widths = [piece.shape[2] for piece in flat]
    stacked = jnp.concatenate(flat, axis=2)
    sizes = [lax.axis_size(name) for name in DP]
    summed = stacked.reshape(stacked.shape[0], *sizes, stacked.shape[2])
    for position in reversed(range(len(DP))):
        if position == len(DP) - 1 and sizes[position] == 2:
            me = lax.axis_index(DP[position])
            major = jnp.moveaxis(summed, 1 + position, 0)
            own = lax.dynamic_index_in_dim(major, me, axis=0, keepdims=False)
            other = lax.dynamic_index_in_dim(major, 1 - me, axis=0, keepdims=False)
            summed = jnp.expand_dims(
                own + lax.ppermute(other, DP[position], [(0, 1), (1, 0)]), 1 + position
            )
            continue
        wire = summed if position == len(DP) - 1 else summed.astype(jnp.bfloat16)
        summed = lax.all_to_all(
            wire, DP[position], split_axis=1 + position, concat_axis=1 + position, tiled=True
        ).astype(jnp.float32).sum(axis=1 + position, keepdims=True)
    summed = summed.reshape(stacked.shape[0], 1, stacked.shape[2])
    outs = []
    start = 0
    for term, width in zip(terms, widths):
        piece = summed[:, 0, start:start + width]
        start += width
        outs.append(piece.reshape(term.shape[0], term.shape[1] // groups, term.shape[2]) * scale)
    return (grad_x, *outs)


def solution(mesh):
    dp = mesh.shape["dp"]
    mp = mesh.shape["mp"]
    sub = (dp // 8, 4, 2) if dp % 8 == 0 else (dp,)
    fine = Mesh(mesh.devices.reshape(*sub, mp), DP[-len(sub):] + ("mp",))
    names = DP[-len(sub):]
    in_specs = (
        P(names, "mp"),
        P(names, "mp"),
        P("mp", None, None),
        P("mp", None, None),
        P("mp", None, None),
        P("mp", None, None),
        P("mp", None, None),
        P("mp", None, None),
    )
    out_specs = (
        P(names, "mp"),
        P("mp", names, None),
        P("mp", names, None),
        P("mp", names, None),
        P("mp", names, None),
        P("mp", names, None),
        P("mp", names, None),
    )
    return jax.shard_map(shards, mesh=fine, in_specs=in_specs, out_specs=out_specs, check_vma=False)
```

```python
import math

import jax
import jax.numpy as jnp
from jax import lax
from jax.sharding import Mesh, PartitionSpec as P

BLK = 128
NBLK = 64
PAIR = 2
FBLK = 448
DP = ("dz", "dx", "dc")


def shards(tokens_in, grad_out, gate_in, gate_out, up_in, up_out, down_in, down_out):
    local_blocks = gate_in.shape[0]
    rows = tokens_in.shape[0]
    groups = lax.axis_size(DP)
    scale = 1.0 / math.sqrt(rows * groups)
    x_blocks = tokens_in.reshape(rows, local_blocks, BLK)
    dy_blocks = grad_out.reshape(rows, local_blocks, BLK)

    def mix_in(weight):
        shaped = weight.reshape(local_blocks, BLK, NBLK, PAIR)
        spread = jnp.einsum("tki,kijp->jkpt", x_blocks, shaped, preferred_element_type=jnp.float32)
        return spread.astype(jnp.bfloat16).reshape(NBLK, local_blocks * PAIR, rows)

    def widen(mixed, weight):
        return jnp.einsum("jct,jco->jot", mixed, weight, preferred_element_type=jnp.float32)

    gate_mid = mix_in(gate_in)
    up_mid = mix_in(up_in)
    back_shaped = down_out.reshape(local_blocks, NBLK, PAIR, BLK)
    back_mid = jnp.einsum(
        "tkr,kjpr->jkpt", dy_blocks, back_shaped, preferred_element_type=jnp.float32
    )
    back_mid = back_mid.astype(jnp.bfloat16).reshape(NBLK, local_blocks * PAIR, rows)
    first_recv = lax.all_to_all(
        jnp.stack([gate_mid, up_mid, back_mid]), "mp", split_axis=1, concat_axis=2, tiled=True
    )
    gate_recv, up_recv, back_recv = first_recv[0], first_recv[1], first_recv[2]
    gate_pre = widen(gate_recv, gate_out)
    up_pre = widen(up_recv, up_out)
    sigmoid_gate = jax.nn.sigmoid(gate_pre)
    activated = gate_pre * sigmoid_gate
    hidden = (activated * up_pre).astype(jnp.bfloat16)
    down_shaped = down_in.reshape(local_blocks, FBLK, NBLK, PAIR)
    down_mid = jnp.einsum("jot,jokp->kjpt", hidden, down_shaped, preferred_element_type=jnp.float32)
    down_mid = down_mid.astype(jnp.bfloat16).reshape(NBLK, local_blocks * PAIR, rows)
    down_recv = lax.all_to_all(down_mid, "mp", split_axis=0, concat_axis=1, tiled=True)
    term_down_out = jnp.einsum(
        "kct,tkr->kcr", down_recv, dy_blocks, preferred_element_type=jnp.float32
    )
    term_down_in = jnp.einsum("jot,jqt->joq", hidden, back_recv, preferred_element_type=jnp.float32)
    hidden_grad = jnp.einsum("joq,jqt->jot", down_in, back_recv, preferred_element_type=jnp.float32)
    gate_grad = (
        hidden_grad * up_pre * sigmoid_gate * (1.0 + gate_pre * (1.0 - sigmoid_gate))
    ).astype(jnp.bfloat16)
    up_grad = (hidden_grad * activated).astype(jnp.bfloat16)
    term_gate_out = jnp.einsum(
        "jct,jot->jco", gate_recv, gate_grad, preferred_element_type=jnp.float32
    )
    term_up_out = jnp.einsum("jct,jot->jco", up_recv, up_grad, preferred_element_type=jnp.float32)

    def narrow(grad, weight):
        shaped = weight.reshape(local_blocks, NBLK, PAIR, FBLK)
        spread = jnp.einsum("jot,jkpo->kjpt", grad, shaped, preferred_element_type=jnp.float32)
        return spread.astype(jnp.bfloat16).reshape(NBLK, local_blocks * PAIR, rows)

    back_recv2 = lax.all_to_all(
        jnp.stack([narrow(gate_grad, gate_out), narrow(up_grad, up_out)]),
        "mp", split_axis=1, concat_axis=2, tiled=True,
    )
    gate_back, up_back = back_recv2[0], back_recv2[1]
    input_grad = jnp.einsum("kio,kot->tki", gate_in, gate_back, preferred_element_type=jnp.float32)
    input_grad = input_grad + jnp.einsum(
        "kio,kot->tki", up_in, up_back, preferred_element_type=jnp.float32
    )
    term_gate_in = jnp.einsum(
        "tki,kot->kio", x_blocks, gate_back, preferred_element_type=jnp.float32
    )
    term_up_in = jnp.einsum("tki,kot->kio", x_blocks, up_back, preferred_element_type=jnp.float32)
    grad_x = input_grad.astype(jnp.bfloat16).reshape(rows, local_blocks * BLK)
    terms = (term_gate_in, term_gate_out, term_up_in, term_up_out, term_down_in, term_down_out)
    flat = [term.reshape(term.shape[0], groups, -1) for term in terms]
    widths = [piece.shape[2] for piece in flat]
    stacked = jnp.concatenate(flat, axis=2)
    sizes = [lax.axis_size(name) for name in DP]
    summed = stacked.reshape(stacked.shape[0], *sizes, stacked.shape[2])
    for position in reversed(range(len(DP))):
        if position == len(DP) - 1 and sizes[position] == 2:
            me = lax.axis_index(DP[position])
            first = lax.index_in_dim(summed, 0, axis=1 + position)
            second = lax.index_in_dim(summed, 1, axis=1 + position)
            own = jnp.where(me == 0, first, second)
            other = jnp.where(me == 0, second, first)
            summed = own + lax.ppermute(other, DP[position], [(0, 1), (1, 0)])
            continue
        wire = summed if position == len(DP) - 1 else summed.astype(jnp.bfloat16)
        summed = lax.all_to_all(
            wire, DP[position], split_axis=1 + position, concat_axis=1 + position, tiled=True
        ).astype(jnp.float32).sum(axis=1 + position, keepdims=True)
    summed = summed.reshape(stacked.shape[0], 1, stacked.shape[2])
    outs = []
    start = 0
    for term, width in zip(terms, widths):
        piece = summed[:, 0, start:start + width]
        start += width
        outs.append(piece.reshape(term.shape[0], term.shape[1] // groups, term.shape[2]) * scale)
    return (grad_x, *outs)


def solution(mesh):
    dp = mesh.shape["dp"]
    mp = mesh.shape["mp"]
    sub = (dp // 8, 4, 2) if dp % 8 == 0 else (dp,)
    fine = Mesh(mesh.devices.reshape(*sub, mp), DP[-len(sub):] + ("mp",))
    names = DP[-len(sub):]
    in_specs = (
        P(names, "mp"),
        P(names, "mp"),
        P("mp", None, None),
        P("mp", None, None),
        P("mp", None, None),
        P("mp", None, None),
        P("mp", None, None),
        P("mp", None, None),
    )
    out_specs = (
        P(names, "mp"),
        P("mp", names, None),
        P("mp", names, None),
        P("mp", names, None),
        P("mp", names, None),
        P("mp", names, None),
        P("mp", names, None),
    )
    return jax.shard_map(shards, mesh=fine, in_specs=in_specs, out_specs=out_specs, check_vma=False)
```

```python
import math

import jax
import jax.numpy as jnp
from jax import lax
from jax.sharding import Mesh, PartitionSpec as P

BLK = 128
NBLK = 64
PAIR = 2
FBLK = 448
DP = ("dz", "dx", "dc")


def shards(tokens_in, grad_out, gate_in, gate_out, up_in, up_out, down_in, down_out):
    local_blocks = gate_in.shape[0]
    rows = tokens_in.shape[0]
    groups = lax.axis_size(DP)
    scale = 1.0 / math.sqrt(rows * groups)
    x_blocks = tokens_in.reshape(rows, local_blocks, BLK)
    dy_blocks = grad_out.reshape(rows, local_blocks, BLK)

    def mix_in(weight):
        shaped = weight.reshape(local_blocks, BLK, NBLK, PAIR)
        spread = jnp.einsum("tki,kijp->jkpt", x_blocks, shaped, preferred_element_type=jnp.float32)
        return spread.astype(jnp.bfloat16).reshape(NBLK, local_blocks * PAIR, rows)

    def widen(mixed, weight):
        return jnp.einsum("jct,jco->jot", mixed, weight, preferred_element_type=jnp.float32)

    gate_mid = mix_in(gate_in)
    up_mid = mix_in(up_in)
    back_shaped = down_out.reshape(local_blocks, NBLK, PAIR, BLK)
    back_mid = jnp.einsum(
        "tkr,kjpr->jkpt", dy_blocks, back_shaped, preferred_element_type=jnp.float32
    )
    back_mid = back_mid.astype(jnp.bfloat16).reshape(NBLK, local_blocks * PAIR, rows)
    first_recv = lax.all_to_all(
        jnp.stack([gate_mid, up_mid, back_mid]), "mp", split_axis=1, concat_axis=2, tiled=True
    )
    gate_recv, up_recv, back_recv = first_recv[0], first_recv[1], first_recv[2]
    gate_pre = widen(gate_recv, gate_out)
    up_pre = widen(up_recv, up_out)
    sigmoid_gate = jax.nn.sigmoid(gate_pre)
    activated = gate_pre * sigmoid_gate
    hidden = (activated * up_pre).astype(jnp.bfloat16)
    down_shaped = down_in.reshape(local_blocks, FBLK, NBLK, PAIR)
    down_mid = jnp.einsum("jot,jokp->kjpt", hidden, down_shaped, preferred_element_type=jnp.float32)
    down_mid = down_mid.astype(jnp.bfloat16).reshape(NBLK, local_blocks * PAIR, rows)
    down_recv = lax.all_to_all(down_mid, "mp", split_axis=0, concat_axis=1, tiled=True)
    term_down_out = jnp.einsum(
        "kct,tkr->kcr", down_recv, dy_blocks, preferred_element_type=jnp.float32
    )
    term_down_in = jnp.einsum("jot,jqt->joq", hidden, back_recv, preferred_element_type=jnp.float32)
    hidden_grad = jnp.einsum("joq,jqt->jot", down_in, back_recv, preferred_element_type=jnp.float32)
    gate_grad = (
        hidden_grad * up_pre * sigmoid_gate * (1.0 + gate_pre * (1.0 - sigmoid_gate))
    ).astype(jnp.bfloat16)
    up_grad = (hidden_grad * activated).astype(jnp.bfloat16)
    term_gate_out = jnp.einsum(
        "jct,jot->jco", gate_recv, gate_grad, preferred_element_type=jnp.float32
    )
    term_up_out = jnp.einsum("jct,jot->jco", up_recv, up_grad, preferred_element_type=jnp.float32)

    def narrow(grad, weight):
        shaped = weight.reshape(local_blocks, NBLK, PAIR, FBLK)
        spread = jnp.einsum("jot,jkpo->kjpt", grad, shaped, preferred_element_type=jnp.float32)
        return spread.astype(jnp.bfloat16).reshape(NBLK, local_blocks * PAIR, rows)

    back_recv2 = lax.all_to_all(
        jnp.stack([narrow(gate_grad, gate_out), narrow(up_grad, up_out)]),
        "mp", split_axis=1, concat_axis=2, tiled=True,
    )
    gate_back, up_back = back_recv2[0], back_recv2[1]
    input_grad = jnp.einsum("kio,kot->tki", gate_in, gate_back, preferred_element_type=jnp.float32)
    input_grad = input_grad + jnp.einsum(
        "kio,kot->tki", up_in, up_back, preferred_element_type=jnp.float32
    )
    term_gate_in = jnp.einsum(
        "tki,kot->kio", x_blocks, gate_back, preferred_element_type=jnp.float32
    )
    term_up_in = jnp.einsum("tki,kot->kio", x_blocks, up_back, preferred_element_type=jnp.float32)
    grad_x = input_grad.astype(jnp.bfloat16).reshape(rows, local_blocks * BLK)
    terms = (term_gate_in, term_gate_out, term_up_in, term_up_out, term_down_in, term_down_out)
    flat = [term.reshape(term.shape[0], groups, -1) for term in terms]
    widths = [piece.shape[2] for piece in flat]
    stacked = jnp.concatenate(flat, axis=2)
    sizes = [lax.axis_size(name) for name in DP]
    summed = stacked.reshape(stacked.shape[0], *sizes, stacked.shape[2])
    for position in reversed(range(len(DP))):
        if position == len(DP) - 1 and sizes[position] == 2:
            me = lax.axis_index(DP[position])
            parts = [
                piece.reshape(piece.shape[0], *sizes, piece.shape[2]) for piece in flat
            ]
            firsts = [lax.index_in_dim(p, 0, axis=1 + position) for p in parts]
            seconds = [lax.index_in_dim(p, 1, axis=1 + position) for p in parts]
            own = jnp.concatenate(
                [jnp.where(me == 0, a, b) for a, b in zip(firsts, seconds)], axis=-1
            )
            other = jnp.concatenate(
                [jnp.where(me == 0, b, a) for a, b in zip(firsts, seconds)], axis=-1
            )
            summed = own + lax.ppermute(other, DP[position], [(0, 1), (1, 0)])
            continue
        wire = summed if position == len(DP) - 1 else summed.astype(jnp.bfloat16)
        summed = lax.all_to_all(
            wire, DP[position], split_axis=1 + position, concat_axis=1 + position, tiled=True
        ).astype(jnp.float32).sum(axis=1 + position, keepdims=True)
    summed = summed.reshape(stacked.shape[0], 1, stacked.shape[2])
    outs = []
    start = 0
    for term, width in zip(terms, widths):
        piece = summed[:, 0, start:start + width]
        start += width
        outs.append(piece.reshape(term.shape[0], term.shape[1] // groups, term.shape[2]) * scale)
    return (grad_x, *outs)


def solution(mesh):
    dp = mesh.shape["dp"]
    mp = mesh.shape["mp"]
    sub = (dp // 8, 4, 2) if dp % 8 == 0 else (dp,)
    fine = Mesh(mesh.devices.reshape(*sub, mp), DP[-len(sub):] + ("mp",))
    names = DP[-len(sub):]
    in_specs = (
        P(names, "mp"),
        P(names, "mp"),
        P("mp", None, None),
        P("mp", None, None),
        P("mp", None, None),
        P("mp", None, None),
        P("mp", None, None),
        P("mp", None, None),
    )
    out_specs = (
        P(names, "mp"),
        P("mp", names, None),
        P("mp", names, None),
        P("mp", names, None),
        P("mp", names, None),
        P("mp", names, None),
        P("mp", names, None),
    )
    return jax.shard_map(shards, mesh=fine, in_specs=in_specs, out_specs=out_specs, check_vma=False)
```

```python
import math

import jax
import jax.numpy as jnp
from jax import lax
from jax.sharding import Mesh, PartitionSpec as P

BLK = 128
NBLK = 64
PAIR = 2
FBLK = 448
DP = ("dz", "dx", "dc")


def shards(tokens_in, grad_out, gate_in, gate_out, up_in, up_out, down_in, down_out):
    local_blocks = gate_in.shape[0]
    rows = tokens_in.shape[0]
    groups = lax.axis_size(DP)
    scale = 1.0 / math.sqrt(rows * groups)
    x_blocks = tokens_in.reshape(rows, local_blocks, BLK)
    dy_blocks = grad_out.reshape(rows, local_blocks, BLK)

    def mix_in(weight):
        shaped = weight.reshape(local_blocks, BLK, NBLK, PAIR)
        spread = jnp.einsum("tki,kijp->jkpt", x_blocks, shaped, preferred_element_type=jnp.float32)
        return spread.astype(jnp.bfloat16).reshape(NBLK, local_blocks * PAIR, rows)

    def widen(mixed, weight):
        return jnp.einsum("jct,jco->jot", mixed, weight, preferred_element_type=jnp.float32)

    gate_mid = mix_in(gate_in)
    up_mid = mix_in(up_in)
    back_shaped = down_out.reshape(local_blocks, NBLK, PAIR, BLK)
    back_mid = jnp.einsum(
        "tkr,kjpr->jkpt", dy_blocks, back_shaped, preferred_element_type=jnp.float32
    )
    back_mid = back_mid.astype(jnp.bfloat16).reshape(NBLK, local_blocks * PAIR, rows)
    first_recv = lax.all_to_all(
        jnp.stack([gate_mid, up_mid, back_mid]), "mp", split_axis=1, concat_axis=2, tiled=True
    )
    gate_recv, up_recv, back_recv = first_recv[0], first_recv[1], first_recv[2]
    gate_pre = widen(gate_recv, gate_out)
    up_pre = widen(up_recv, up_out)
    sigmoid_gate = jax.nn.sigmoid(gate_pre)
    activated = gate_pre * sigmoid_gate
    hidden = (activated * up_pre).astype(jnp.bfloat16)
    down_shaped = down_in.reshape(local_blocks, FBLK, NBLK, PAIR)
    down_mid = jnp.einsum("jot,jokp->kjpt", hidden, down_shaped, preferred_element_type=jnp.float32)
    down_mid = down_mid.astype(jnp.bfloat16).reshape(NBLK, local_blocks * PAIR, rows)
    down_recv = lax.all_to_all(down_mid, "mp", split_axis=0, concat_axis=1, tiled=True)
    term_down_out = jnp.einsum(
        "kct,tkr->kcr", down_recv, dy_blocks, preferred_element_type=jnp.float32
    )
    term_down_in = jnp.einsum("jot,jqt->joq", hidden, back_recv, preferred_element_type=jnp.float32)
    hidden_grad = jnp.einsum("joq,jqt->jot", down_in, back_recv, preferred_element_type=jnp.float32)
    gate_grad = (
        hidden_grad * up_pre * sigmoid_gate * (1.0 + gate_pre * (1.0 - sigmoid_gate))
    ).astype(jnp.bfloat16)
    up_grad = (hidden_grad * activated).astype(jnp.bfloat16)
    term_gate_out = jnp.einsum(
        "jct,jot->jco", gate_recv, gate_grad, preferred_element_type=jnp.float32
    )
    term_up_out = jnp.einsum("jct,jot->jco", up_recv, up_grad, preferred_element_type=jnp.float32)

    def narrow(grad, weight):
        shaped = weight.reshape(local_blocks, NBLK, PAIR, FBLK)
        spread = jnp.einsum("jot,jkpo->kjpt", grad, shaped, preferred_element_type=jnp.float32)
        return spread.astype(jnp.bfloat16).reshape(NBLK, local_blocks * PAIR, rows)

    back_recv2 = lax.all_to_all(
        jnp.stack([narrow(gate_grad, gate_out), narrow(up_grad, up_out)]),
        "mp", split_axis=1, concat_axis=2, tiled=True,
    )
    gate_back, up_back = back_recv2[0], back_recv2[1]
    input_grad = jnp.einsum("kio,kot->tki", gate_in, gate_back, preferred_element_type=jnp.float32)
    input_grad = input_grad + jnp.einsum(
        "kio,kot->tki", up_in, up_back, preferred_element_type=jnp.float32
    )
    term_gate_in = jnp.einsum(
        "tki,kot->kio", x_blocks, gate_back, preferred_element_type=jnp.float32
    )
    term_up_in = jnp.einsum("tki,kot->kio", x_blocks, up_back, preferred_element_type=jnp.float32)
    grad_x = input_grad.astype(jnp.bfloat16).reshape(rows, local_blocks * BLK)
    terms = (term_gate_in, term_gate_out, term_up_in, term_up_out, term_down_in, term_down_out)
    flat = [(term * scale).reshape(term.shape[0], groups, -1) for term in terms]
    widths = [piece.shape[2] for piece in flat]
    stacked = jnp.concatenate(flat, axis=2)
    sizes = [lax.axis_size(name) for name in DP]
    summed = stacked.reshape(stacked.shape[0], *sizes, stacked.shape[2])
    for position in reversed(range(len(DP))):
        if position == len(DP) - 1 and sizes[position] == 2:
            me = lax.axis_index(DP[position])
            first = lax.index_in_dim(summed, 0, axis=1 + position)
            second = lax.index_in_dim(summed, 1, axis=1 + position)
            own = jnp.where(me == 0, first, second)
            other = jnp.where(me == 0, second, first)
            summed = own + lax.ppermute(other, DP[position], [(0, 1), (1, 0)])
            continue
        wire = summed if position == len(DP) - 1 else summed.astype(jnp.bfloat16)
        summed = lax.all_to_all(
            wire, DP[position], split_axis=1 + position, concat_axis=1 + position, tiled=True
        ).astype(jnp.float32).sum(axis=1 + position, keepdims=True)
    summed = summed.reshape(stacked.shape[0], 1, stacked.shape[2])
    outs = []
    start = 0
    for term, width in zip(terms, widths):
        piece = summed[:, 0, start:start + width]
        start += width
        outs.append(piece.reshape(term.shape[0], term.shape[1] // groups, term.shape[2]))
    return (grad_x, *outs)


def solution(mesh):
    dp = mesh.shape["dp"]
    mp = mesh.shape["mp"]
    sub = (dp // 8, 4, 2) if dp % 8 == 0 else (dp,)
    fine = Mesh(mesh.devices.reshape(*sub, mp), DP[-len(sub):] + ("mp",))
    names = DP[-len(sub):]
    in_specs = (
        P(names, "mp"),
        P(names, "mp"),
        P("mp", None, None),
        P("mp", None, None),
        P("mp", None, None),
        P("mp", None, None),
        P("mp", None, None),
        P("mp", None, None),
    )
    out_specs = (
        P(names, "mp"),
        P("mp", names, None),
        P("mp", names, None),
        P("mp", names, None),
        P("mp", names, None),
        P("mp", names, None),
        P("mp", names, None),
    )
    return jax.shard_map(shards, mesh=fine, in_specs=in_specs, out_specs=out_specs, check_vma=False)
```
